512 devices in a mesh: seq: 128 (over y, z, core), tp: 4 (over x).
Axes of the slice: x: 4, y: 8, z: 8, core: 2. Of those that a mesh axis runs over, the one named last changes fastest.
Arguments:
- tokens: bfloat16 [32768, 1280], P('seq', 'tp'), may hold values from -6 to 6
- first_gain: float32 [1280], replicated, may hold values from 0.1 to 1.9
- w_query: bfloat16 [1280, 1280], P(None, 'tp')
- w_key: bfloat16 [1280, 1280], P(None, 'tp')
- w_value: bfloat16 [1280, 1280], P(None, 'tp'), may hold values from -0.15625 to 0.15625
- w_out: bfloat16 [1280, 1280], P('tp'), may hold values from -0.625 to 0.625
- segment_ids: int32 [32768], P('seq'), may hold values from 0 to 191, never falling along the last dimension, each value on 1 to 512 neighbouring positions
- keep_mask: int32 [32768], P('seq'), may hold values 0 or 1
- merge_gain: float32 [1280], replicated, may hold values from 0.1 to 1.9
- w_merge: bfloat16 [5120, 640], P('tp'), may hold values from -0.078125 to 0.078125
- merge_index: int32 [8192, 4], P('seq'), may hold values from 0 to 32767, as said below
- destination: int32 [8192], P('seq'), may hold values from 0 to 8191, as said below
Outputs:
- delivered: bfloat16 [8192, 640], P('seq', 'tp')
The draws below stay inside these ranges and needn't reach their ends.
Inputs may be any that keep to these rules, and one draw needn't show every extreme that they name: `segment_ids`: segment numbers never fall along the tokens; each picture or clip holds 1 to 512 tokens and one holds exactly 512. `merge_index`: the four entries of merged row m are different tokens of the device that holds row m, that is of rows (m // 64) * 256 to that plus 256 - 1; every token lies in exactly one group. `destination`: a permutation of the merged rows. The owner of row m is destination[m] // 64; the 64 rows of each device go to exactly 32 owners, exactly 2 rows to each.
All inputs are finite; a program needn't handle non-finite values. No bound on the sum of `keep_mask` on one device may be relied on, other than what follows from the above.
Results may differ from the reference program's by a relative error of at most 0.022.
Values may be sent and summed in bfloat16 or wider, within the bound.
No kernel may reach another device: no remote copies, remote signals or barrier semaphores. Data moves between devices by JAX's collectives and lax.ppermute only.
A program may use at most 64 MiB of HBM per device.

```python
import math
import jax
import jax.numpy as jnp
import numpy as np
from jax import lax

D = 1280
HEADS = 16
HD = 80
OUT = 640
TOK_DEV = 256
TOKENS = 32768
MROWS_DEV = 64
MTOT = 8192
MOST = 512
COUNT = 192
CAP = 2
GROUPS_SENT = 32
N_SEQ = 128


def query_base(key):
    return jax.random.normal(jax.random.fold_in(key, 11), (D, D), jnp.float32) * D ** (-0.5)


def draw_w_query(key, part):
    return query_base(key).astype(jnp.bfloat16)


def draw_w_key(key, part):
    noise = jax.random.normal(jax.random.fold_in(key, 12), (D, D), jnp.float32) * D ** (-0.5)
    return noise.astype(jnp.bfloat16)


def shuffled(key, count, length):
    split_keys = jax.random.split(key, count)
    return jax.vmap(lambda sub_key: jax.random.permutation(sub_key, length))(split_keys).astype(jnp.int32)


def draw_merge_index(key, part):
    orders = shuffled(jax.random.fold_in(key, 21), N_SEQ, TOK_DEV)
    offsets = (jnp.arange(N_SEQ, dtype=jnp.int32) * TOK_DEV)[:, None]
    return (orders + offsets).reshape(MTOT, 4)


def draw_destination(key, part):
    first = jax.random.permutation(jax.random.fold_in(key, 31), N_SEQ).astype(jnp.int32)
    second = jax.random.permutation(jax.random.fold_in(key, 32), N_SEQ).astype(jnp.int32)
    shifts = jax.random.permutation(jax.random.fold_in(key, 33), N_SEQ).astype(jnp.int32)[:GROUPS_SENT]
    owners = first[(second[:, None] + shifts[None, :]) % N_SEQ]
    slot_orders = shuffled(jax.random.fold_in(key, 34), N_SEQ, MROWS_DEV)
    row_orders = shuffled(jax.random.fold_in(key, 35), N_SEQ, MROWS_DEV)
    within = jnp.arange(GROUPS_SENT, dtype=jnp.int32)[:, None] * CAP + jnp.arange(CAP, dtype=jnp.int32)[None, :]
    slots = slot_orders[owners[:, :, None], within[None, :, :]]
    targets = (owners[:, :, None] * MROWS_DEV + slots).reshape(N_SEQ, MROWS_DEV)
    result = jnp.zeros((N_SEQ, MROWS_DEV), jnp.int32)
    result = result.at[jnp.arange(N_SEQ, dtype=jnp.int32)[:, None], row_orders].set(targets)
    return result.reshape(MTOT)


def set_ends(drawn, rng, low, largest):
    longest = drawn.shape.index(max(drawn.shape))
    spots = []
    for shift in (0, 1):
        where = [jax.random.randint(jax.random.fold_in(rng, axis), (), 0, length) for axis, length in enumerate(drawn.shape)]
        where[longest] = (where[longest] + shift) % drawn.shape[longest]
        spots.append(tuple(where))
    return drawn.at[spots[0]].set(low).at[spots[1]].set(largest)


def block_levels(rng, extent, cuts, least, high):
    def one(dim, shards_of):
        draws = jax.random.uniform(jax.random.fold_in(jax.random.fold_in(rng, 6), dim), (shards_of,), jnp.float32, least / len(cuts), high / len(cuts))
        return jnp.repeat(jnp.exp(draws), extent[dim] // shards_of).reshape((-1,) + (1,) * (len(extent) - dim - 1))

    level = one(*cuts[0])
    for cut in cuts[1:]:
        level = level * one(*cut)
    return level


def split_up(amount, total, most, skew):
    portions = [(1 << 20) // math.isqrt(grade ** skew) + 1 for grade in range(2, amount + 1)]
    surplus, counts = total - most - (amount - 1), [1] * (amount - 1)
    while surplus > 0:
        candidates = [i for i in range(amount - 1) if counts[i] < most]
        whole, remaining = sum([portions[i] for i in candidates]), surplus
        for i in candidates:
            addition = min(most - counts[i], max(1, remaining * portions[i] // whole), surplus)
            counts[i] = counts[i] + addition
            surplus = surplus - addition
    return np.array([most] + counts)


def uneven_parts(key, count, total, most, slope):
    if count == 2:
        one = jax.random.randint(key, (), max(1, total - most), min(most, total - 1) + 1)
        return jnp.stack([one, total - one])
    tallies = jnp.asarray(split_up(count, total, most, slope), jnp.int32)
    couples = (count - 1) // 2
    giver, receiver = tallies[1:1 + 2 * couples:2], tallies[2:2 + 2 * couples:2]
    slack = jnp.minimum(giver - 1, most - receiver)
    moved = jax.random.randint(jax.random.fold_in(key, 1), (couples,), 0, 1 << 20) % (slack + 1)
    tallies = tallies.at[1:1 + 2 * couples:2].set(giver - moved).at[2:2 + 2 * couples:2].set(receiver + moved)
    return tallies[jax.random.permutation(jax.random.fold_in(key, 2), count)]


def centred(stream_key, extent, deviation, reach, shards=(), kind=jnp.bfloat16):
    drawn = jax.random.normal(stream_key, extent, jnp.float32) * deviation
    if len(shards) > 0:
        drawn = block_levels(stream_key, extent, shards, -0.22, 0.18) * drawn
    return jnp.clip(drawn, min=-reach, max=reach).astype(kind)


def setup_inputs(seed: int = 0) -> dict:
    streams_of = jax.random.split(jax.random.key(seed), 13)
    return {
        "tokens": centred(streams_of[0], (TOKENS, D), 1.0, 6.0, ((0, 128), (1, 4))),
        "first_gain": jnp.clip(1.0 + 0.18 * jax.random.normal(streams_of[1], (D,), jnp.float32), 0.1, 1.9),
        "w_query": draw_w_query(jax.random.fold_in(streams_of[12], 71), 0),
        "w_key": draw_w_key(jax.random.fold_in(streams_of[12], 71), 0),
        "w_value": centred(streams_of[4], (D, D), D ** -0.5, 0.15625, ((1, 4),)),
        "w_out": centred(streams_of[5], (D, D), HD ** -0.5, 0.625, ((0, 4),)),
        "segment_ids": jnp.searchsorted(jnp.cumsum(uneven_parts(streams_of[6], COUNT, TOKENS, MOST, 2)), jnp.arange(TOKENS), side="right").astype(jnp.int32),
        "keep_mask": set_ends((jax.random.randint(streams_of[7], (TOKENS,), 0, 8) < 7).astype(jnp.int32), jax.random.fold_in(streams_of[7], 1), 0, 1),
        "merge_gain": jnp.clip(1.0 + 0.18 * jax.random.normal(streams_of[8], (D,), jnp.float32), 0.1, 1.9),
        "w_merge": centred(streams_of[9], (4 * D, OUT), (4 * D) ** -0.5, 0.078125, ((0, 4),)),
        "merge_index": draw_merge_index(jax.random.fold_in(streams_of[12], 71), 0),
        "destination": draw_destination(jax.random.fold_in(streams_of[12], 71), 0),
    }


EPS = 1e-06

def layer_norm(activations, norm_gain):
    activations = activations.astype(jnp.float32)
    row_mean = lax.optimization_barrier(jnp.mean(activations, axis=-1, keepdims=True))
    centered = activations - row_mean
    variance = lax.optimization_barrier(jnp.mean(centered * centered, axis=-1, keepdims=True))
    return centered * lax.rsqrt(variance + EPS) * norm_gain.astype(jnp.float32)

def reference(tokens, first_gain, w_query, w_key, w_value, w_out, segment_ids, keep_mask, merge_gain, w_merge, merge_index, destination):
    normed = layer_norm(tokens, first_gain).astype(jnp.bfloat16)
    queries = jnp.dot(normed, w_query, preferred_element_type=jnp.float32).astype(jnp.bfloat16)
    key_rows = jnp.dot(normed, w_key, preferred_element_type=jnp.float32).astype(jnp.bfloat16)
    value_rows = jnp.dot(normed, w_value, preferred_element_type=jnp.float32).astype(jnp.bfloat16)
    code_query = segment_ids + 1
    code_key = jnp.where(keep_mask > 0, segment_ids + 1, 0)
    margin = 2 * TOK_DEV
    key_padded = jnp.pad(key_rows, ((margin, margin), (0, 0)))
    value_padded = jnp.pad(value_rows, ((margin, margin), (0, 0)))
    code_padded = jnp.pad(code_key, ((margin, margin),))
    score_scale = HD ** (-0.5)
    window = 5 * TOK_DEV

    def attend_block(block_index):
        block_start = (block_index * TOK_DEV).astype(jnp.int32)
        query_block = lax.dynamic_slice_in_dim(queries, block_start, TOK_DEV, 0)
        key_block = lax.dynamic_slice_in_dim(key_padded, block_start, window, 0)
        value_block = lax.dynamic_slice_in_dim(value_padded, block_start, window, 0)
        query_codes = lax.dynamic_slice_in_dim(code_query, block_start, TOK_DEV, 0)
        key_codes = lax.dynamic_slice_in_dim(code_padded, block_start, window, 0)
        query_pos = jnp.arange(TOK_DEV)[:, None]
        key_pos = jnp.arange(window)[None, :]
        allowed = (query_codes[:, None] == key_codes[None, :]) | (key_pos == query_pos + margin)
        query_heads = query_block.reshape(TOK_DEV, HEADS, HD).astype(jnp.float32)
        key_heads = key_block.reshape(window, HEADS, HD).astype(jnp.float32)
        value_heads = value_block.reshape(window, HEADS, HD).astype(jnp.float32)
        scores = jnp.einsum('qhd,khd->hqk', query_heads, key_heads) * score_scale
        scores = jnp.where(allowed[None], scores, -1e+30)
        row_max = lax.optimization_barrier(jnp.max(scores, axis=-1, keepdims=True))
        exponent = jnp.exp(scores - row_max)
        row_total = lax.optimization_barrier(jnp.sum(exponent, axis=-1, keepdims=True))
        weights = (exponent / row_total).astype(jnp.bfloat16)
        result = jnp.einsum('hqk,khd->qhd', weights.astype(jnp.float32), value_heads)
        return result.reshape(TOK_DEV, D).astype(jnp.bfloat16)
    attended = lax.map(attend_block, jnp.arange(N_SEQ, dtype=jnp.int32)).reshape(TOKENS, D)
    mixed_sum = jnp.dot(attended, w_out, preferred_element_type=jnp.float32)
    updated = tokens.astype(jnp.float32) + mixed_sum
    merged_norm = layer_norm(updated, merge_gain).astype(jnp.bfloat16)
    grouped = jnp.take(merged_norm, merge_index, axis=0).reshape(MTOT, 4 * D)
    projected = jnp.dot(grouped, w_merge, preferred_element_type=jnp.float32).astype(jnp.bfloat16)
    delivered = jnp.zeros((MTOT, OUT), jnp.bfloat16).at[destination].set(projected)
    return delivered
```

```python
import jax
import jax.numpy as jnp
from jax import lax
from jax.sharding import PartitionSpec as P

HD = 80
CAP = 2


EPS = 1e-06


def from_behind(shard, axis, by):
    length = lax.axis_size(axis)
    pairs = [(i, i + by) for i in range(length) if 0 <= i + by < length]
    return lax.ppermute(shard, axis, pairs)


def layer_norm(activations, norm_gain):
    activations = activations.astype(jnp.float32)
    row_mean = jnp.mean(activations, axis=-1, keepdims=True)
    centered = activations - row_mean
    variance = jnp.mean(centered * centered, axis=-1, keepdims=True)
    return centered * lax.rsqrt(variance + EPS) * norm_gain


def body(
    tokens,
    first_gain,
    w_query,
    w_key,
    w_value,
    w_out,
    segment_ids,
    keep_mask,
    merge_gain,
    w_merge,
    merge_index,
    destination,
):
    row_count = tokens.shape[0]
    local_width = w_query.shape[1]
    heads_here = local_width // HD
    tp_size = lax.axis_size("tp")
    seq_size = lax.axis_size("seq")
    gathered = lax.all_gather(tokens, "tp", axis=1, tiled=True)
    normed = layer_norm(gathered, first_gain).astype(jnp.bfloat16)
    queries = jnp.dot(normed, w_query, preferred_element_type=jnp.float32).astype(jnp.bfloat16)
    key_rows = jnp.dot(normed, w_key, preferred_element_type=jnp.float32).astype(jnp.bfloat16)
    value_rows = jnp.dot(normed, w_value, preferred_element_type=jnp.float32).astype(jnp.bfloat16)
    paired = jnp.concatenate([key_rows, value_rows], axis=1)
    code_query = segment_ids + 1
    code_key = jnp.where(keep_mask > 0, code_query, 0)
    pair_list = [paired]
    code_list = [code_key]
    for offset in (1, 2, -1, -2):
        moved_pair, moved_code = from_behind((paired, code_key), "seq", offset)
        pair_list.append(moved_pair)
        code_list.append(moved_code)
    all_pairs = jnp.concatenate(pair_list, axis=0)
    all_codes = jnp.concatenate(code_list, axis=0)
    window = all_pairs.shape[0]
    key_heads = all_pairs[:, :local_width].reshape(window, heads_here, HD)
    value_heads = all_pairs[:, local_width:].reshape(window, heads_here, HD)
    query_heads = queries.reshape(row_count, heads_here, HD)
    score_scale = HD ** (-0.5)
    scores = (
        jnp.einsum("qhd,khd->hqk", query_heads, key_heads, preferred_element_type=jnp.float32)
        * score_scale
    )
    query_pos = jnp.arange(row_count)[:, None]
    key_pos = jnp.arange(window)[None, :]
    allowed = (code_query[:, None] == all_codes[None, :]) | (key_pos == query_pos)
    scores = jnp.where(allowed[None], scores, -1e30)
    row_max = jnp.max(scores, axis=-1, keepdims=True)
    exponent = jnp.exp(scores - row_max)
    row_total = jnp.sum(exponent, axis=-1, keepdims=True)
    weights = (exponent / row_total).astype(jnp.bfloat16)
    attended = jnp.einsum("hqk,khd->qhd", weights, value_heads, preferred_element_type=jnp.float32)
    attended = attended.reshape(row_count, local_width).astype(jnp.bfloat16)

    position = lax.axis_index("tp")
    seq_index = lax.axis_index("seq")
    local_index = merge_index - seq_index * row_count
    order = local_index.T.reshape(row_count)
    attended_sorted = jnp.take(attended, order, axis=0)
    partial_sum = jnp.dot(attended_sorted, w_out, preferred_element_type=jnp.float32)
    mixed_sum = lax.psum_scatter(
        partial_sum.astype(jnp.bfloat16), "tp", scatter_dimension=0, tiled=True
    ).astype(jnp.float32)
    column = lax.dynamic_slice_in_dim(local_index, position, 1, 1)[:, 0]
    residual = jnp.take(gathered, column, axis=0)
    updated = residual.astype(jnp.float32) + mixed_sum
    picked = layer_norm(updated, merge_gain).astype(jnp.bfloat16)
    partial_proj = jnp.dot(picked, w_merge, preferred_element_type=jnp.float32)
    projected = lax.psum_scatter(
        partial_proj.astype(jnp.bfloat16), "tp", scatter_dimension=1, tiled=True
    )
    slot_count = projected.shape[0]
    width = projected.shape[1]

    owner = destination // slot_count
    slot = destination - owner * slot_count
    lane = jnp.arange(slot_count)
    same_owner = owner[:, None] == owner[None, :]
    earlier = lane[None, :] < lane[:, None]
    rank = jnp.sum(jnp.where(same_owner & earlier, 1, 0), axis=1)
    send_pos = owner * CAP + rank
    target = jnp.arange(seq_size * CAP)
    send_hot = (send_pos[None, :] == target[:, None]).astype(jnp.bfloat16)
    send_rows = jnp.dot(send_hot, projected, preferred_element_type=jnp.float32)
    send_rows = send_rows.astype(jnp.bfloat16).reshape(seq_size, CAP, width)
    slot_code = (slot + 1).astype(jnp.float32)
    send_slot = jnp.dot(send_hot.astype(jnp.float32), slot_code, precision=lax.Precision.HIGHEST)
    slot_row = jnp.zeros((seq_size, 1, width), jnp.bfloat16)
    slot_row = slot_row.at[:, 0, :CAP].set(send_slot.reshape(seq_size, CAP).astype(jnp.bfloat16))
    send_buf = jnp.concatenate([send_rows, slot_row], axis=1).reshape(seq_size * (CAP + 1), width)
    recv = lax.all_to_all(send_buf, "seq", 0, 0, tiled=True).reshape(seq_size, CAP + 1, width)
    recv_rows = recv[:, :CAP, :].reshape(seq_size * CAP, width)
    recv_slot = recv[:, CAP, :CAP].reshape(seq_size * CAP).astype(jnp.int32) - 1
    recv_hot = (recv_slot[None, :] == lane[:, None]).astype(jnp.bfloat16)
    delivered = jnp.dot(recv_hot, recv_rows, preferred_element_type=jnp.float32)
    return delivered.astype(jnp.bfloat16)


def solution(mesh):
    return jax.shard_map(
        body,
        mesh=mesh,
        in_specs=(
            P("seq", "tp"),
            P(),
            P(None, "tp"),
            P(None, "tp"),
            P(None, "tp"),
            P("tp", None),
            P("seq"),
            P("seq"),
            P(),
            P("tp", None),
            P("seq", None),
            P("seq"),
        ),
        out_specs=P("seq", "tp"),
        check_vma=False,
    )
```

```python
import jax
import jax.numpy as jnp
from jax import lax
from jax.sharding import PartitionSpec as P

HD = 80
CAP = 2


EPS = 1e-06


def from_behind(shard, axis, by):
    length = lax.axis_size(axis)
    pairs = [(i, i + by) for i in range(length) if 0 <= i + by < length]
    return lax.ppermute(shard, axis, pairs)


def around(shard, axis, by):
    length = lax.axis_size(axis)
    pairs = [(i, (i + by) % length) for i in range(length)]
    return lax.ppermute(shard, axis, pairs)


def layer_norm(activations, norm_gain):
    activations = activations.astype(jnp.float32)
    row_mean = jnp.mean(activations, axis=-1, keepdims=True)
    centered = activations - row_mean
    variance = jnp.mean(centered * centered, axis=-1, keepdims=True)
    return centered * lax.rsqrt(variance + EPS) * norm_gain


def body(
    tokens,
    first_gain,
    w_query,
    w_key,
    w_value,
    w_out,
    segment_ids,
    keep_mask,
    merge_gain,
    w_merge,
    merge_index,
    destination,
):
    row_count = tokens.shape[0]
    local_width = w_query.shape[1]
    heads_here = local_width // HD
    tp_size = lax.axis_size("tp")
    seq_size = lax.axis_size("seq")
    position = lax.axis_index("tp")
    seq_index = lax.axis_index("seq")

    blocks = [tokens] + [around(tokens, "tp", -k) for k in range(1, tp_size)]
    rotated = jnp.concatenate(blocks + blocks, axis=1)
    start = ((tp_size - position) % tp_size) * tokens.shape[1]
    gathered = lax.dynamic_slice_in_dim(rotated, start, tp_size * tokens.shape[1], 1)

    normed = layer_norm(gathered, first_gain).astype(jnp.bfloat16)
    queries = jnp.dot(normed, w_query, preferred_element_type=jnp.float32).astype(jnp.bfloat16)
    key_rows = jnp.dot(normed, w_key, preferred_element_type=jnp.float32).astype(jnp.bfloat16)
    value_rows = jnp.dot(normed, w_value, preferred_element_type=jnp.float32).astype(jnp.bfloat16)
    code_query = segment_ids + 1
    code_key = jnp.where(keep_mask > 0, code_query, 0)
    pair_width = 2 * local_width
    code_block = jnp.zeros((8, pair_width), jnp.bfloat16)
    code_block = code_block.at[0, :row_count].set(code_key.astype(jnp.bfloat16))
    paired = jnp.concatenate([jnp.concatenate([key_rows, value_rows], axis=1), code_block], axis=0)
    pair_list = [paired]
    for offset in (1, 2, -1, -2):
        pair_list.append(from_behind(paired, "seq", offset))
    all_pairs = jnp.concatenate([p[:row_count] for p in pair_list], axis=0)
    all_codes = jnp.concatenate(
        [code_key] + [p[row_count, :row_count].astype(jnp.int32) for p in pair_list[1:]], axis=0
    )
    window = all_pairs.shape[0]
    key_heads = all_pairs[:, :local_width].reshape(window, heads_here, HD)
    value_heads = all_pairs[:, local_width:].reshape(window, heads_here, HD)
    query_heads = queries.reshape(row_count, heads_here, HD)
    score_scale = HD ** (-0.5)
    scores = (
        jnp.einsum("qhd,khd->hqk", query_heads, key_heads, preferred_element_type=jnp.float32)
        * score_scale
    )
    query_pos = jnp.arange(row_count)[:, None]
    key_pos = jnp.arange(window)[None, :]
    allowed = (code_query[:, None] == all_codes[None, :]) | (key_pos == query_pos)
    scores = jnp.where(allowed[None], scores, -1e30)
    row_max = jnp.max(scores, axis=-1, keepdims=True)
    exponent = jnp.exp(scores - row_max)
    row_total = jnp.sum(exponent, axis=-1, keepdims=True)
    weights = (exponent / row_total).astype(jnp.bfloat16)
    attended = jnp.einsum("hqk,khd->qhd", weights, value_heads, preferred_element_type=jnp.float32)
    attended = attended.reshape(row_count, local_width).astype(jnp.bfloat16)

    local_index = merge_index - seq_index * row_count
    rotated_index = jnp.concatenate([local_index, local_index], axis=1)
    rotated_index = lax.dynamic_slice_in_dim(rotated_index, position, tp_size, 1)
    order = rotated_index.T.reshape(row_count)
    attended_sorted = jnp.take(attended, order, axis=0)
    partial_sum = jnp.dot(attended_sorted, w_out, preferred_element_type=jnp.float32)
    partial_sum = partial_sum.astype(jnp.bfloat16)
    chunk = row_count // tp_size
    mixed_sum = partial_sum[:chunk].astype(jnp.float32)
    for k in range(1, tp_size):
        mixed_sum = mixed_sum + around(partial_sum[k * chunk:(k + 1) * chunk], "tp", k).astype(jnp.float32)
    column = rotated_index[:, 0]
    residual = jnp.take(gathered, column, axis=0)
    updated = residual.astype(jnp.float32) + mixed_sum
    picked = layer_norm(updated, merge_gain).astype(jnp.bfloat16)
    partial_proj = jnp.dot(picked, w_merge, preferred_element_type=jnp.float32)
    partial_proj = partial_proj.astype(jnp.bfloat16)
    width = partial_proj.shape[1] // tp_size
    doubled = jnp.concatenate([partial_proj, partial_proj], axis=1)
    projected = lax.dynamic_slice_in_dim(doubled, position * width, width, 1).astype(jnp.float32)
    for k in range(1, tp_size):
        piece = lax.dynamic_slice_in_dim(doubled, (position + k) * width, width, 1)
        projected = projected + around(piece, "tp", k).astype(jnp.float32)
    projected = projected.astype(jnp.bfloat16)
    slot_count = projected.shape[0]

    owner = destination // slot_count
    slot = destination - owner * slot_count
    lane = jnp.arange(slot_count)
    same_owner = owner[:, None] == owner[None, :]
    earlier = lane[None, :] < lane[:, None]
    rank = jnp.sum(jnp.where(same_owner & earlier, 1, 0), axis=1)
    send_pos = owner * CAP + rank
    target = jnp.arange(seq_size * CAP)
    send_hot = (send_pos[None, :] == target[:, None]).astype(jnp.bfloat16)
    send_rows = jnp.dot(send_hot, projected, preferred_element_type=jnp.float32)
    send_rows = send_rows.astype(jnp.bfloat16).reshape(seq_size, CAP, width)
    slot_code = (slot + 1).astype(jnp.float32)
    send_slot = jnp.dot(send_hot.astype(jnp.float32), slot_code, precision=lax.Precision.HIGHEST)
    slot_row = jnp.zeros((seq_size, 1, width), jnp.bfloat16)
    slot_row = slot_row.at[:, 0, :CAP].set(send_slot.reshape(seq_size, CAP).astype(jnp.bfloat16))
    send_buf = jnp.concatenate([send_rows, slot_row], axis=1).reshape(seq_size * (CAP + 1), width)
    recv = lax.all_to_all(send_buf, "seq", 0, 0, tiled=True).reshape(seq_size, CAP + 1, width)
    recv_rows = recv[:, :CAP, :].reshape(seq_size * CAP, width)
    recv_slot = recv[:, CAP, :CAP].reshape(seq_size * CAP).astype(jnp.int32) - 1
    recv_hot = (recv_slot[None, :] == lane[:, None]).astype(jnp.bfloat16)
    delivered = jnp.dot(recv_hot, recv_rows, preferred_element_type=jnp.float32)
    return delivered.astype(jnp.bfloat16)


def solution(mesh):
    return jax.shard_map(
        body,
        mesh=mesh,
        in_specs=(
            P("seq", "tp"),
            P(),
            P(None, "tp"),
            P(None, "tp"),
            P(None, "tp"),
            P("tp", None),
            P("seq"),
            P("seq"),
            P(),
            P("tp", None),
            P("seq", None),
            P("seq"),
        ),
        out_specs=P("seq", "tp"),
        check_vma=False,
    )
```

```python
import jax
import jax.numpy as jnp
from jax import lax
from jax.sharding import PartitionSpec as P

HD = 80
CAP = 2


EPS = 1e-06


def from_behind(shard, axis, by):
    length = lax.axis_size(axis)
    pairs = [(i, i + by) for i in range(length) if 0 <= i + by < length]
    return lax.ppermute(shard, axis, pairs)


def layer_norm(activations, norm_gain):
    activations = activations.astype(jnp.float32)
    row_mean = jnp.mean(activations, axis=-1, keepdims=True)
    centered = activations - row_mean
    variance = jnp.mean(centered * centered, axis=-1, keepdims=True)
    return centered * lax.rsqrt(variance + EPS) * norm_gain


def body(
    tokens,
    first_gain,
    w_query,
    w_key,
    w_value,
    w_out,
    segment_ids,
    keep_mask,
    merge_gain,
    w_merge,
    merge_index,
    destination,
):
    row_count = tokens.shape[0]
    local_width = w_query.shape[1]
    heads_here = local_width // HD
    tp_size = lax.axis_size("tp")
    seq_size = lax.axis_size("seq")
    position = lax.axis_index("tp")
    seq_index = lax.axis_index("seq")

    gathered = lax.all_to_all(
        jnp.concatenate([tokens] * tp_size, axis=1), "tp", 1, 1, tiled=True
    )

    normed = layer_norm(gathered, first_gain).astype(jnp.bfloat16)
    queries = jnp.dot(normed, w_query, preferred_element_type=jnp.float32).astype(jnp.bfloat16)
    key_rows = jnp.dot(normed, w_key, preferred_element_type=jnp.float32).astype(jnp.bfloat16)
    value_rows = jnp.dot(normed, w_value, preferred_element_type=jnp.float32).astype(jnp.bfloat16)
    code_query = segment_ids + 1
    code_key = jnp.where(keep_mask > 0, code_query, 0)
    pair_width = 2 * local_width
    code_block = jnp.zeros((8, pair_width), jnp.bfloat16)
    code_block = code_block.at[0, :row_count].set(code_key.astype(jnp.bfloat16))
    paired = jnp.concatenate([jnp.concatenate([key_rows, value_rows], axis=1), code_block], axis=0)
    pair_list = [paired]
    for offset in (1, 2, -1, -2):
        pair_list.append(from_behind(paired, "seq", offset))
    all_pairs = jnp.concatenate([p[:row_count] for p in pair_list], axis=0)
    all_codes = jnp.concatenate(
        [code_key] + [p[row_count, :row_count].astype(jnp.int32) for p in pair_list[1:]], axis=0
    )
    window = all_pairs.shape[0]
    key_heads = all_pairs[:, :local_width].reshape(window, heads_here, HD)
    value_heads = all_pairs[:, local_width:].reshape(window, heads_here, HD)
    query_heads = queries.reshape(row_count, heads_here, HD)
    score_scale = HD ** (-0.5)
    scores = (
        jnp.einsum("qhd,khd->hqk", query_heads, key_heads, preferred_element_type=jnp.float32)
        * score_scale
    )
    query_pos = jnp.arange(row_count)[:, None]
    key_pos = jnp.arange(window)[None, :]
    allowed = (code_query[:, None] == all_codes[None, :]) | (key_pos == query_pos)
    scores = jnp.where(allowed[None], scores, -1e30)
    row_max = jnp.max(scores, axis=-1, keepdims=True)
    exponent = jnp.exp(scores - row_max)
    row_total = jnp.sum(exponent, axis=-1, keepdims=True)
    weights = (exponent / row_total).astype(jnp.bfloat16)
    attended = jnp.einsum("hqk,khd->qhd", weights, value_heads, preferred_element_type=jnp.float32)
    attended = attended.reshape(row_count, local_width).astype(jnp.bfloat16)

    local_index = merge_index - seq_index * row_count
    order = local_index.T.reshape(row_count)
    attended_sorted = jnp.take(attended, order, axis=0)
    partial_sum = jnp.dot(attended_sorted, w_out, preferred_element_type=jnp.float32)
    partial_sum = partial_sum.astype(jnp.bfloat16)
    chunk = row_count // tp_size
    pieces = lax.all_to_all(partial_sum, "tp", 0, 0, tiled=True)
    mixed_sum = jnp.sum(pieces.reshape(tp_size, chunk, -1).astype(jnp.float32), axis=0)
    column = lax.dynamic_slice_in_dim(local_index, position, 1, 1)[:, 0]
    residual = jnp.take(gathered, column, axis=0)
    updated = residual.astype(jnp.float32) + mixed_sum
    picked = layer_norm(updated, merge_gain).astype(jnp.bfloat16)
    partial_proj = jnp.dot(picked, w_merge, preferred_element_type=jnp.float32)
    partial_proj = partial_proj.astype(jnp.bfloat16)
    width = partial_proj.shape[1] // tp_size
    proj_pieces = lax.all_to_all(partial_proj, "tp", 1, 0, tiled=True)
    projected = jnp.sum(proj_pieces.reshape(tp_size, chunk, width).astype(jnp.float32), axis=0)
    projected = projected.astype(jnp.bfloat16)
    slot_count = projected.shape[0]

    owner = destination // slot_count
    slot = destination - owner * slot_count
    lane = jnp.arange(slot_count)
    same_owner = owner[:, None] == owner[None, :]
    earlier = lane[None, :] < lane[:, None]
    rank = jnp.sum(jnp.where(same_owner & earlier, 1, 0), axis=1)
    send_pos = owner * CAP + rank
    target = jnp.arange(seq_size * CAP)
    send_hot = (send_pos[None, :] == target[:, None]).astype(jnp.bfloat16)
    send_rows = jnp.dot(send_hot, projected, preferred_element_type=jnp.float32)
    send_rows = send_rows.astype(jnp.bfloat16).reshape(seq_size, CAP, width)
    slot_code = (slot + 1).astype(jnp.float32)
    send_slot = jnp.dot(send_hot.astype(jnp.float32), slot_code, precision=lax.Precision.HIGHEST)
    slot_row = jnp.zeros((seq_size, 1, width), jnp.bfloat16)
    slot_row = slot_row.at[:, 0, :CAP].set(send_slot.reshape(seq_size, CAP).astype(jnp.bfloat16))
    send_buf = jnp.concatenate([send_rows, slot_row], axis=1).reshape(seq_size * (CAP + 1), width)
    recv = lax.all_to_all(send_buf, "seq", 0, 0, tiled=True).reshape(seq_size, CAP + 1, width)
    recv_rows = recv[:, :CAP, :].reshape(seq_size * CAP, width)
    recv_slot = recv[:, CAP, :CAP].reshape(seq_size * CAP).astype(jnp.int32) - 1
    recv_hot = (recv_slot[None, :] == lane[:, None]).astype(jnp.bfloat16)
    delivered = jnp.dot(recv_hot, recv_rows, preferred_element_type=jnp.float32)
    return delivered.astype(jnp.bfloat16)


def solution(mesh):
    return jax.shard_map(
        body,
        mesh=mesh,
        in_specs=(
            P("seq", "tp"),
            P(),
            P(None, "tp"),
            P(None, "tp"),
            P(None, "tp"),
            P("tp", None),
            P("seq"),
            P("seq"),
            P(),
            P("tp", None),
            P("seq", None),
            P("seq"),
        ),
        out_specs=P("seq", "tp"),
        check_vma=False,
    )
```

```python
import jax
import jax.numpy as jnp
from jax import lax
from jax.sharding import PartitionSpec as P

HD = 80
CAP = 2


EPS = 1e-06


def from_behind(shard, axis, by):
    length = lax.axis_size(axis)
    pairs = [(i, i + by) for i in range(length) if 0 <= i + by < length]
    return lax.ppermute(shard, axis, pairs)


def layer_norm(activations, norm_gain):
    activations = activations.astype(jnp.float32)
    row_mean = jnp.mean(activations, axis=-1, keepdims=True)
    centered = activations - row_mean
    variance = jnp.mean(centered * centered, axis=-1, keepdims=True)
    return centered * lax.rsqrt(variance + EPS) * norm_gain


def body(
    tokens,
    first_gain,
    w_query,
    w_key,
    w_value,
    w_out,
    segment_ids,
    keep_mask,
    merge_gain,
    w_merge,
    merge_index,
    destination,
):
    row_count = tokens.shape[0]
    local_width = w_query.shape[1]
    heads_here = local_width // HD
    tp_size = lax.axis_size("tp")
    seq_size = lax.axis_size("seq")
    position = lax.axis_index("tp")
    seq_index = lax.axis_index("seq")

    gathered = lax.all_to_all(
        jnp.concatenate([tokens] * tp_size, axis=1), "tp", 1, 1, tiled=True
    )

    normed = layer_norm(gathered, first_gain).astype(jnp.bfloat16)
    queries = jnp.dot(normed, w_query, preferred_element_type=jnp.float32).astype(jnp.bfloat16)
    key_rows = jnp.dot(normed, w_key, preferred_element_type=jnp.float32).astype(jnp.bfloat16)
    value_rows = jnp.dot(normed, w_value, preferred_element_type=jnp.float32).astype(jnp.bfloat16)
    code_query = segment_ids + 1
    code_key = jnp.where(keep_mask > 0, code_query, 0)
    pair_width = 2 * local_width
    code_block = jnp.zeros((8, pair_width), jnp.bfloat16)
    code_block = code_block.at[0, :row_count].set(code_key.astype(jnp.bfloat16))
    paired = jnp.concatenate([jnp.concatenate([key_rows, value_rows], axis=1), code_block], axis=0)
    pair_list = [paired]
    for offset in (1, 2, -1, -2):
        pair_list.append(from_behind(paired, "seq", offset))
    all_pairs = jnp.concatenate([p[:row_count] for p in pair_list], axis=0)
    all_codes = jnp.concatenate(
        [code_key] + [p[row_count, :row_count].astype(jnp.int32) for p in pair_list[1:]], axis=0
    )
    window = all_pairs.shape[0]
    key_heads = all_pairs[:, :local_width].reshape(window, heads_here, HD)
    value_heads = all_pairs[:, local_width:].reshape(window, heads_here, HD)
    query_heads = queries.reshape(row_count, heads_here, HD)
    score_scale = HD ** (-0.5)
    scores = (
        jnp.einsum("qhd,khd->hqk", query_heads, key_heads, preferred_element_type=jnp.float32)
        * score_scale
    )
    query_pos = jnp.arange(row_count)[:, None]
    key_pos = jnp.arange(window)[None, :]
    allowed = (code_query[:, None] == all_codes[None, :]) | (key_pos == query_pos)
    scores = jnp.where(allowed[None], scores, -1e30)
    row_max = jnp.max(scores, axis=-1, keepdims=True)
    exponent = jnp.exp(scores - row_max)
    row_total = jnp.sum(exponent, axis=-1, keepdims=True)
    weights = (exponent / row_total).astype(jnp.bfloat16)
    attended = jnp.einsum("hqk,khd->qhd", weights, value_heads, preferred_element_type=jnp.float32)
    attended = attended.reshape(row_count, local_width).astype(jnp.bfloat16)

    local_index = merge_index - seq_index * row_count
    order = local_index.T.reshape(row_count)
    attended_sorted = jnp.take(attended, order, axis=0)
    partial_sum = jnp.dot(attended_sorted, w_out, preferred_element_type=jnp.float32)
    partial_sum = partial_sum.astype(jnp.bfloat16)
    chunk = row_count // tp_size
    pieces = lax.all_to_all(partial_sum, "tp", 0, 0, tiled=True)
    mixed_sum = jnp.sum(pieces.reshape(tp_size, chunk, -1).astype(jnp.float32), axis=0)
    column = lax.dynamic_slice_in_dim(local_index, position, 1, 1)[:, 0]
    residual = jnp.take(gathered, column, axis=0)
    updated = residual.astype(jnp.float32) + mixed_sum
    picked = layer_norm(updated, merge_gain).astype(jnp.bfloat16)
    partial_proj = jnp.dot(picked, w_merge, preferred_element_type=jnp.float32)
    partial_proj = partial_proj.astype(jnp.bfloat16)
    width = partial_proj.shape[1] // tp_size
    slot_count = partial_proj.shape[0]

    owner = destination // slot_count
    slot = destination - owner * slot_count
    lane = jnp.arange(slot_count)
    same_owner = owner[:, None] == owner[None, :]
    earlier = lane[None, :] < lane[:, None]
    rank = jnp.sum(jnp.where(same_owner & earlier, 1, 0), axis=1)
    send_pos = owner * CAP + rank
    target = jnp.arange(seq_size * CAP)
    send_hot = (send_pos[None, :] == target[:, None]).astype(jnp.bfloat16)
    send_rows = jnp.dot(send_hot, partial_proj, preferred_element_type=jnp.float32)
    send_rows = send_rows.astype(jnp.bfloat16).reshape(seq_size, CAP, tp_size, width)
    send_rows = jnp.transpose(send_rows, (0, 2, 1, 3))
    slot_code = (slot + 1).astype(jnp.float32)
    send_slot = jnp.dot(send_hot.astype(jnp.float32), slot_code, precision=lax.Precision.HIGHEST)
    slot_row = jnp.zeros((seq_size, 1, width), jnp.bfloat16)
    slot_row = slot_row.at[:, 0, :CAP].set(send_slot.reshape(seq_size, CAP).astype(jnp.bfloat16))
    slot_row = jnp.broadcast_to(slot_row[:, None], (seq_size, tp_size, 1, width))
    send_buf = jnp.concatenate([send_rows, slot_row], axis=2)
    send_buf = send_buf.reshape(seq_size * tp_size * (CAP + 1), width)
    recv = lax.all_to_all(send_buf, ("seq", "tp"), 0, 0, tiled=True)
    recv = recv.reshape(seq_size, tp_size, CAP + 1, width)
    recv_rows = jnp.sum(recv[:, :, :CAP, :].astype(jnp.float32), axis=1)
    recv_rows = recv_rows.astype(jnp.bfloat16).reshape(seq_size * CAP, width)
    recv_slot = recv[:, 0, CAP, :CAP].reshape(seq_size * CAP).astype(jnp.int32) - 1
    recv_hot = (recv_slot[None, :] == lane[:, None]).astype(jnp.bfloat16)
    delivered = jnp.dot(recv_hot, recv_rows, preferred_element_type=jnp.float32)
    return delivered.astype(jnp.bfloat16)


def solution(mesh):
    return jax.shard_map(
        body,
        mesh=mesh,
        in_specs=(
            P("seq", "tp"),
            P(),
            P(None, "tp"),
            P(None, "tp"),
            P(None, "tp"),
            P("tp", None),
            P("seq"),
            P("seq"),
            P(),
            P("tp", None),
            P("seq", None),
            P("seq"),
        ),
        out_specs=P("seq", "tp"),
        check_vma=False,
    )
```

```python
import jax
import jax.numpy as jnp
from jax import lax
from jax.sharding import PartitionSpec as P

HD = 80
CAP = 2


EPS = 1e-06


def from_behind(shard, axis, by):
    length = lax.axis_size(axis)
    pairs = [(i, i + by) for i in range(length) if 0 <= i + by < length]
    return lax.ppermute(shard, axis, pairs)


def layer_norm(activations, norm_gain):
    activations = activations.astype(jnp.float32)
    row_mean = jnp.mean(activations, axis=-1, keepdims=True)
    centered = activations - row_mean
    variance = jnp.mean(centered * centered, axis=-1, keepdims=True)
    return centered * lax.rsqrt(variance + EPS) * norm_gain


def body(
    tokens,
    first_gain,
    w_query,
    w_key,
    w_value,
    w_out,
    segment_ids,
    keep_mask,
    merge_gain,
    w_merge,
    merge_index,
    destination,
):
    row_count = tokens.shape[0]
    local_width = w_query.shape[1]
    heads_here = local_width // HD
    tp_size = lax.axis_size("tp")
    seq_size = lax.axis_size("seq")
    position = lax.axis_index("tp")
    seq_index = lax.axis_index("seq")

    local_index = merge_index - seq_index * row_count
    order = local_index.T.reshape(row_count)
    tokens = jnp.take(tokens, order, axis=0)
    segment_ids = jnp.take(segment_ids, order, axis=0)
    keep_mask = jnp.take(keep_mask, order, axis=0)
    gathered = lax.all_to_all(
        jnp.concatenate([tokens] * tp_size, axis=1), "tp", 1, 1, tiled=True
    )

    normed = layer_norm(gathered, first_gain).astype(jnp.bfloat16)
    queries = jnp.dot(normed, w_query, preferred_element_type=jnp.float32).astype(jnp.bfloat16)
    key_rows = jnp.dot(normed, w_key, preferred_element_type=jnp.float32).astype(jnp.bfloat16)
    value_rows = jnp.dot(normed, w_value, preferred_element_type=jnp.float32).astype(jnp.bfloat16)
    code_query = segment_ids + 1
    code_key = jnp.where(keep_mask > 0, code_query, 0)
    pair_width = 2 * local_width
    code_block = jnp.zeros((8, pair_width), jnp.bfloat16)
    code_block = code_block.at[0, :row_count].set(code_key.astype(jnp.bfloat16))
    paired = jnp.concatenate([jnp.concatenate([key_rows, value_rows], axis=1), code_block], axis=0)
    pair_list = [paired]
    for offset in (1, 2, -1, -2):
        pair_list.append(from_behind(paired, "seq", offset))
    all_pairs = jnp.concatenate([p[:row_count] for p in pair_list], axis=0)
    all_codes = jnp.concatenate(
        [code_key] + [p[row_count, :row_count].astype(jnp.int32) for p in pair_list[1:]], axis=0
    )
    window = all_pairs.shape[0]
    key_heads = all_pairs[:, :local_width].reshape(window, heads_here, HD)
    value_heads = all_pairs[:, local_width:].reshape(window, heads_here, HD)
    query_heads = queries.reshape(row_count, heads_here, HD)
    score_scale = HD ** (-0.5)
    scores = (
        jnp.einsum("qhd,khd->hqk", query_heads, key_heads, preferred_element_type=jnp.float32)
        * score_scale
    )
    query_pos = jnp.arange(row_count)[:, None]
    key_pos = jnp.arange(window)[None, :]
    allowed = (code_query[:, None] == all_codes[None, :]) | (key_pos == query_pos)
    scores = jnp.where(allowed[None], scores, -1e30)
    row_max = jnp.max(scores, axis=-1, keepdims=True)
    exponent = jnp.exp(scores - row_max)
    row_total = jnp.sum(exponent, axis=-1, keepdims=True)
    weights = (exponent / row_total).astype(jnp.bfloat16)
    attended = jnp.einsum("hqk,khd->qhd", weights, value_heads, preferred_element_type=jnp.float32)
    attended = attended.astype(jnp.bfloat16)
    out_heads = w_out.reshape(heads_here, HD, w_out.shape[1])
    partial_sum = jnp.einsum("qhd,hdn->qn", attended, out_heads, preferred_element_type=jnp.float32)
    partial_sum = partial_sum.astype(jnp.bfloat16)
    chunk = row_count // tp_size
    pieces = lax.all_to_all(partial_sum, "tp", 0, 0, tiled=True)
    mixed_sum = jnp.sum(pieces.reshape(tp_size, chunk, -1).astype(jnp.float32), axis=0)
    residual = lax.dynamic_slice_in_dim(gathered, position * chunk, chunk, 0)
    updated = residual.astype(jnp.float32) + mixed_sum
    picked = layer_norm(updated, merge_gain).astype(jnp.bfloat16)
    partial_proj = jnp.dot(picked, w_merge, preferred_element_type=jnp.float32)
    partial_proj = partial_proj.astype(jnp.bfloat16)
    width = partial_proj.shape[1] // tp_size
    proj_pieces = lax.all_to_all(partial_proj, "tp", 1, 0, tiled=True)
    projected = jnp.sum(proj_pieces.reshape(tp_size, chunk, width).astype(jnp.float32), axis=0)
    projected = projected.astype(jnp.bfloat16)
    slot_count = projected.shape[0]

    owner = destination // slot_count
    slot = destination - owner * slot_count
    lane = jnp.arange(slot_count)
    same_owner = owner[:, None] == owner[None, :]
    earlier = lane[None, :] < lane[:, None]
    rank = jnp.sum(jnp.where(same_owner & earlier, 1, 0), axis=1)
    send_pos = owner * CAP + rank
    target = jnp.arange(seq_size * CAP)
    send_hot = (send_pos[None, :] == target[:, None]).astype(jnp.bfloat16)
    send_rows = jnp.dot(send_hot, projected, preferred_element_type=jnp.float32)
    send_rows = send_rows.astype(jnp.bfloat16).reshape(seq_size, CAP, width)
    slot_code = (slot + 1).astype(jnp.float32)
    send_slot = jnp.dot(send_hot.astype(jnp.float32), slot_code, precision=lax.Precision.HIGHEST)
    slot_row = jnp.zeros((seq_size, 1, width), jnp.bfloat16)
    slot_row = slot_row.at[:, 0, :CAP].set(send_slot.reshape(seq_size, CAP).astype(jnp.bfloat16))
    send_buf = jnp.concatenate([send_rows, slot_row], axis=1).reshape(seq_size * (CAP + 1), width)
    recv = lax.all_to_all(send_buf, "seq", 0, 0, tiled=True).reshape(seq_size, CAP + 1, width)
    recv_rows = recv[:, :CAP, :].reshape(seq_size * CAP, width)
    recv_slot = recv[:, CAP, :CAP].reshape(seq_size * CAP).astype(jnp.int32) - 1
    recv_hot = (recv_slot[None, :] == lane[:, None]).astype(jnp.bfloat16)
    delivered = jnp.dot(recv_hot, recv_rows, preferred_element_type=jnp.float32)
    return delivered.astype(jnp.bfloat16)


def solution(mesh):
    return jax.shard_map(
        body,
        mesh=mesh,
        in_specs=(
            P("seq", "tp"),
            P(),
            P(None, "tp"),
            P(None, "tp"),
            P(None, "tp"),
            P("tp", None),
            P("seq"),
            P("seq"),
            P(),
            P("tp", None),
            P("seq", None),
            P("seq"),
        ),
        out_specs=P("seq", "tp"),
        check_vma=False,
    )
```

```python
import functools

import jax
import jax.numpy as jnp
from jax import lax
from jax.experimental import pallas as pl
from jax.experimental.pallas import tpu as pltpu
from jax.sharding import PartitionSpec as P

HD = 80
CAP = 2


EPS = 1e-06


def from_behind(shard, axis, by):
    length = lax.axis_size(axis)
    pairs = [(i, i + by) for i in range(length) if 0 <= i + by < length]
    return lax.ppermute(shard, axis, pairs)


def attn_kernel(heads, rows, qcode_ref, q_ref, b0, b1, b2, b3, b4, out_ref):
    blocks = (b0, b1, b2, b3, b4)
    scale = HD ** (-0.5)
    qcode = qcode_ref[...]
    width = heads * HD
    row_id = lax.broadcasted_iota(jnp.int32, (rows, rows), 0)
    col_id = lax.broadcasted_iota(jnp.int32, (rows, rows), 1)
    diag = row_id == col_id
    masks = []
    for b, blk in enumerate(blocks):
        kcode = blk[rows:rows + 1, 0:rows].astype(jnp.float32)
        m = qcode == kcode
        if b == 0:
            m = m | diag
        masks.append(m)
    for h in range(heads):
        q = q_ref[:, h * HD:(h + 1) * HD]
        scores = []
        for b, blk in enumerate(blocks):
            k = blk[0:rows, h * HD:(h + 1) * HD]
            s = lax.dot_general(q, k, (((1,), (1,)), ((), ())), preferred_element_type=jnp.float32) * scale
            scores.append(jnp.where(masks[b], s, -1e30))
        row_max = scores[0].max(axis=1, keepdims=True)
        for s in scores[1:]:
            row_max = jnp.maximum(row_max, s.max(axis=1, keepdims=True))
        exps = [jnp.exp(s - row_max) for s in scores]
        total = exps[0].sum(axis=1, keepdims=True)
        for e in exps[1:]:
            total = total + e.sum(axis=1, keepdims=True)
        acc = None
        for b, blk in enumerate(blocks):
            w = (exps[b] / total).astype(jnp.bfloat16)
            v = blk[0:rows, width + h * HD:width + (h + 1) * HD]
            p = jnp.dot(w, v, preferred_element_type=jnp.float32)
            acc = p if acc is None else acc + p
        out_ref[:, h * HD:(h + 1) * HD] = acc.astype(out_ref.dtype)


def attention(qcode, q, blocks):
    rows, width = q.shape
    heads = width // HD
    vmem = pl.BlockSpec(memory_space=pltpu.VMEM)
    flops = 2 * 2 * heads * rows * rows * len(blocks) * HD
    return pl.pallas_call(
        functools.partial(attn_kernel, heads, rows),
        out_shape=jax.ShapeDtypeStruct((rows, width), jnp.bfloat16),
        in_specs=[vmem] * (2 + len(blocks)),
        out_specs=vmem,
        cost_estimate=pl.CostEstimate(
            flops=flops,
            transcendentals=heads * rows * rows * len(blocks),
            bytes_accessed=sum(b.size * 2 for b in blocks) + q.size * 4,
        ),
    )(qcode, q, *blocks)


def layer_norm(activations, norm_gain):
    activations = activations.astype(jnp.float32)
    row_mean = jnp.mean(activations, axis=-1, keepdims=True)
    centered = activations - row_mean
    variance = jnp.mean(centered * centered, axis=-1, keepdims=True)
    return centered * lax.rsqrt(variance + EPS) * norm_gain


def body(
    tokens,
    first_gain,
    w_query,
    w_key,
    w_value,
    w_out,
    segment_ids,
    keep_mask,
    merge_gain,
    w_merge,
    merge_index,
    destination,
):
    row_count = tokens.shape[0]
    local_width = w_query.shape[1]
    heads_here = local_width // HD
    tp_size = lax.axis_size("tp")
    seq_size = lax.axis_size("seq")
    position = lax.axis_index("tp")
    seq_index = lax.axis_index("seq")

    gathered = lax.all_to_all(
        jnp.concatenate([tokens] * tp_size, axis=1), "tp", 1, 1, tiled=True
    )

    normed = layer_norm(gathered, first_gain).astype(jnp.bfloat16)
    queries = jnp.dot(normed, w_query, preferred_element_type=jnp.float32).astype(jnp.bfloat16)
    key_rows = jnp.dot(normed, w_key, preferred_element_type=jnp.float32).astype(jnp.bfloat16)
    value_rows = jnp.dot(normed, w_value, preferred_element_type=jnp.float32).astype(jnp.bfloat16)
    code_query = segment_ids + 1
    code_key = jnp.where(keep_mask > 0, code_query, 0)
    pair_width = 2 * local_width
    code_block = jnp.zeros((8, pair_width), jnp.bfloat16)
    code_block = code_block.at[0, :row_count].set(code_key.astype(jnp.bfloat16))
    paired = jnp.concatenate([jnp.concatenate([key_rows, value_rows], axis=1), code_block], axis=0)
    pair_list = [paired]
    for offset in (1, 2, -1, -2):
        pair_list.append(from_behind(paired, "seq", offset))
    query_code = code_query.astype(jnp.float32)[:, None]
    attended = attention(query_code, queries, pair_list)

    local_index = merge_index - seq_index * row_count
    order = local_index.T.reshape(row_count)
    attended_sorted = jnp.take(attended, order, axis=0)
    partial_sum = jnp.dot(attended_sorted, w_out, preferred_element_type=jnp.float32)
    partial_sum = partial_sum.astype(jnp.bfloat16)
    chunk = row_count // tp_size
    pieces = lax.all_to_all(partial_sum, "tp", 0, 0, tiled=True)
    mixed_sum = jnp.sum(pieces.reshape(tp_size, chunk, -1).astype(jnp.float32), axis=0)
    column = lax.dynamic_slice_in_dim(local_index, position, 1, 1)[:, 0]
    residual = jnp.take(gathered, column, axis=0)
    updated = residual.astype(jnp.float32) + mixed_sum
    picked = layer_norm(updated, merge_gain).astype(jnp.bfloat16)
    partial_proj = jnp.dot(picked, w_merge, preferred_element_type=jnp.float32)
    partial_proj = partial_proj.astype(jnp.bfloat16)
    width = partial_proj.shape[1] // tp_size
    proj_pieces = lax.all_to_all(partial_proj, "tp", 1, 0, tiled=True)
    projected = jnp.sum(proj_pieces.reshape(tp_size, chunk, width).astype(jnp.float32), axis=0)
    projected = projected.astype(jnp.bfloat16)
    slot_count = projected.shape[0]

    owner = destination // slot_count
    slot = destination - owner * slot_count
    lane = jnp.arange(slot_count)
    same_owner = owner[:, None] == owner[None, :]
    earlier = lane[None, :] < lane[:, None]
    rank = jnp.sum(jnp.where(same_owner & earlier, 1, 0), axis=1)
    send_pos = owner * CAP + rank
    target = jnp.arange(seq_size * CAP)
    send_hot = (send_pos[None, :] == target[:, None]).astype(jnp.bfloat16)
    send_rows = jnp.dot(send_hot, projected, preferred_element_type=jnp.float32)
    send_rows = send_rows.astype(jnp.bfloat16).reshape(seq_size, CAP, width)
    slot_code = (slot + 1).astype(jnp.float32)
    send_slot = jnp.dot(send_hot.astype(jnp.float32), slot_code, precision=lax.Precision.HIGHEST)
    slot_row = jnp.zeros((seq_size, 1, width), jnp.bfloat16)
    slot_row = slot_row.at[:, 0, :CAP].set(send_slot.reshape(seq_size, CAP).astype(jnp.bfloat16))
    send_buf = jnp.concatenate([send_rows, slot_row], axis=1).reshape(seq_size * (CAP + 1), width)
    recv = lax.all_to_all(send_buf, "seq", 0, 0, tiled=True).reshape(seq_size, CAP + 1, width)
    recv_rows = recv[:, :CAP, :].reshape(seq_size * CAP, width)
    recv_slot = recv[:, CAP, :CAP].reshape(seq_size * CAP).astype(jnp.int32) - 1
    recv_hot = (recv_slot[None, :] == lane[:, None]).astype(jnp.bfloat16)
    delivered = jnp.dot(recv_hot, recv_rows, preferred_element_type=jnp.float32)
    return delivered.astype(jnp.bfloat16)


def solution(mesh):
    return jax.shard_map(
        body,
        mesh=mesh,
        in_specs=(
            P("seq", "tp"),
            P(),
            P(None, "tp"),
            P(None, "tp"),
            P(None, "tp"),
            P("tp", None),
            P("seq"),
            P("seq"),
            P(),
            P("tp", None),
            P("seq", None),
            P("seq"),
        ),
        out_specs=P("seq", "tp"),
        check_vma=False,
    )
```

```python
import functools

import jax
import jax.numpy as jnp
from jax import lax
from jax.experimental import pallas as pl
from jax.experimental.pallas import tpu as pltpu
from jax.sharding import PartitionSpec as P

HD = 80
CAP = 2


EPS = 1e-06


def from_behind(shard, axis, by):
    length = lax.axis_size(axis)
    pairs = [(i, i + by) for i in range(length) if 0 <= i + by < length]
    return lax.ppermute(shard, axis, pairs)


def attn_kernel(heads, rows, qcode_ref, order_ref, q_ref, w_ref, b0, b1, b2, b3, b4, out_ref):
    blocks = (b0, b1, b2, b3, b4)
    scale = HD ** (-0.5)
    qcode = qcode_ref[...]
    width = heads * HD
    row_id = lax.broadcasted_iota(jnp.int32, (rows, rows), 0)
    col_id = lax.broadcasted_iota(jnp.int32, (rows, rows), 1)
    diag = row_id == col_id
    masks = []
    for b, blk in enumerate(blocks):
        kcode = blk[rows:rows + 1, 0:rows].astype(jnp.float32)
        m = qcode == kcode
        if b == 0:
            m = m | diag
        masks.append(m)
    pick = (order_ref[...] == col_id).astype(jnp.bfloat16)
    mixed = None
    for h in range(heads):
        q = q_ref[:, h * HD:(h + 1) * HD]
        scores = []
        for b, blk in enumerate(blocks):
            k = blk[0:rows, h * HD:(h + 1) * HD]
            s = lax.dot_general(q, k, (((1,), (1,)), ((), ())), preferred_element_type=jnp.float32) * scale
            scores.append(jnp.where(masks[b], s, -1e30))
        row_max = scores[0].max(axis=1, keepdims=True)
        for s in scores[1:]:
            row_max = jnp.maximum(row_max, s.max(axis=1, keepdims=True))
        exps = [jnp.exp(s - row_max) for s in scores]
        total = exps[0].sum(axis=1, keepdims=True)
        for e in exps[1:]:
            total = total + e.sum(axis=1, keepdims=True)
        acc = None
        for b, blk in enumerate(blocks):
            w = (exps[b] / total).astype(jnp.bfloat16)
            v = blk[0:rows, width + h * HD:width + (h + 1) * HD]
            p = jnp.dot(w, v, preferred_element_type=jnp.float32)
            acc = p if acc is None else acc + p
        ordered = jnp.dot(pick, acc.astype(jnp.bfloat16), preferred_element_type=jnp.float32)
        part = jnp.dot(
            ordered.astype(jnp.bfloat16), w_ref[h * HD:(h + 1) * HD, :],
            preferred_element_type=jnp.float32,
        )
        mixed = part if mixed is None else mixed + part
    out_ref[...] = mixed.astype(out_ref.dtype)


def attention(qcode, order, q, w_out, blocks):
    rows, width = q.shape
    heads = width // HD
    out_width = w_out.shape[1]
    vmem = pl.BlockSpec(memory_space=pltpu.VMEM)
    flops = 2 * 2 * heads * rows * rows * len(blocks) * HD
    flops += 2 * rows * rows * width + 2 * rows * width * out_width
    return pl.pallas_call(
        functools.partial(attn_kernel, heads, rows),
        out_shape=jax.ShapeDtypeStruct((rows, out_width), jnp.bfloat16),
        in_specs=[vmem] * (4 + len(blocks)),
        out_specs=vmem,
        cost_estimate=pl.CostEstimate(
            flops=flops,
            transcendentals=heads * rows * rows * len(blocks),
            bytes_accessed=sum(b.size * 2 for b in blocks) + q.size * 2 + w_out.size * 2 + rows * out_width * 2,
        ),
    )(qcode, order, q, w_out, *blocks)


def layer_norm(activations, norm_gain):
    activations = activations.astype(jnp.float32)
    row_mean = jnp.mean(activations, axis=-1, keepdims=True)
    centered = activations - row_mean
    variance = jnp.mean(centered * centered, axis=-1, keepdims=True)
    return centered * lax.rsqrt(variance + EPS) * norm_gain


def body(
    tokens,
    first_gain,
    w_query,
    w_key,
    w_value,
    w_out,
    segment_ids,
    keep_mask,
    merge_gain,
    w_merge,
    merge_index,
    destination,
):
    row_count = tokens.shape[0]
    local_width = w_query.shape[1]
    heads_here = local_width // HD
    tp_size = lax.axis_size("tp")
    seq_size = lax.axis_size("seq")
    position = lax.axis_index("tp")
    seq_index = lax.axis_index("seq")

    gathered = lax.all_to_all(
        jnp.concatenate([tokens] * tp_size, axis=1), "tp", 1, 1, tiled=True
    )

    normed = layer_norm(gathered, first_gain).astype(jnp.bfloat16)
    queries = jnp.dot(normed, w_query, preferred_element_type=jnp.float32).astype(jnp.bfloat16)
    key_rows = jnp.dot(normed, w_key, preferred_element_type=jnp.float32).astype(jnp.bfloat16)
    value_rows = jnp.dot(normed, w_value, preferred_element_type=jnp.float32).astype(jnp.bfloat16)
    code_query = segment_ids + 1
    code_key = jnp.where(keep_mask > 0, code_query, 0)
    pair_width = 2 * local_width
    code_block = jnp.zeros((8, pair_width), jnp.bfloat16)
    code_block = code_block.at[0, :row_count].set(code_key.astype(jnp.bfloat16))
    paired = jnp.concatenate([jnp.concatenate([key_rows, value_rows], axis=1), code_block], axis=0)
    pair_list = [paired]
    for offset in (1, 2, -1, -2):
        pair_list.append(from_behind(paired, "seq", offset))
    query_code = code_query.astype(jnp.float32)[:, None]
    local_index = merge_index - seq_index * row_count
    order = local_index.T.reshape(row_count)
    partial_sum = attention(query_code, order[:, None], queries, w_out, pair_list)
    chunk = row_count // tp_size
    pieces = lax.all_to_all(partial_sum, "tp", 0, 0, tiled=True)
    mixed_sum = jnp.sum(pieces.reshape(tp_size, chunk, -1).astype(jnp.float32), axis=0)
    column = lax.dynamic_slice_in_dim(local_index, position, 1, 1)[:, 0]
    residual = jnp.take(gathered, column, axis=0)
    updated = residual.astype(jnp.float32) + mixed_sum
    picked = layer_norm(updated, merge_gain).astype(jnp.bfloat16)
    partial_proj = jnp.dot(picked, w_merge, preferred_element_type=jnp.float32)
    partial_proj = partial_proj.astype(jnp.bfloat16)
    width = partial_proj.shape[1] // tp_size
    proj_pieces = lax.all_to_all(partial_proj, "tp", 1, 0, tiled=True)
    projected = jnp.sum(proj_pieces.reshape(tp_size, chunk, width).astype(jnp.float32), axis=0)
    projected = projected.astype(jnp.bfloat16)
    slot_count = projected.shape[0]

    owner = destination // slot_count
    slot = destination - owner * slot_count
    lane = jnp.arange(slot_count)
    same_owner = owner[:, None] == owner[None, :]
    earlier = lane[None, :] < lane[:, None]
    rank = jnp.sum(jnp.where(same_owner & earlier, 1, 0), axis=1)
    send_pos = owner * CAP + rank
    target = jnp.arange(seq_size * CAP)
    send_hot = (send_pos[None, :] == target[:, None]).astype(jnp.bfloat16)
    send_rows = jnp.dot(send_hot, projected, preferred_element_type=jnp.float32)
    send_rows = send_rows.astype(jnp.bfloat16).reshape(seq_size, CAP, width)
    slot_code = (slot + 1).astype(jnp.float32)
    send_slot = jnp.dot(send_hot.astype(jnp.float32), slot_code, precision=lax.Precision.HIGHEST)
    slot_row = jnp.zeros((seq_size, 1, width), jnp.bfloat16)
    slot_row = slot_row.at[:, 0, :CAP].set(send_slot.reshape(seq_size, CAP).astype(jnp.bfloat16))
    send_buf = jnp.concatenate([send_rows, slot_row], axis=1).reshape(seq_size * (CAP + 1), width)
    recv = lax.all_to_all(send_buf, "seq", 0, 0, tiled=True).reshape(seq_size, CAP + 1, width)
    recv_rows = recv[:, :CAP, :].reshape(seq_size * CAP, width)
    recv_slot = recv[:, CAP, :CAP].reshape(seq_size * CAP).astype(jnp.int32) - 1
    recv_hot = (recv_slot[None, :] == lane[:, None]).astype(jnp.bfloat16)
    delivered = jnp.dot(recv_hot, recv_rows, preferred_element_type=jnp.float32)
    return delivered.astype(jnp.bfloat16)


def solution(mesh):
    return jax.shard_map(
        body,
        mesh=mesh,
        in_specs=(
            P("seq", "tp"),
            P(),
            P(None, "tp"),
            P(None, "tp"),
            P(None, "tp"),
            P("tp", None),
            P("seq"),
            P("seq"),
            P(),
            P("tp", None),
            P("seq", None),
            P("seq"),
        ),
        out_specs=P("seq", "tp"),
        check_vma=False,
    )
```

```python
import functools

import jax
import jax.numpy as jnp
from jax import lax
from jax.experimental import pallas as pl
from jax.experimental.pallas import tpu as pltpu
from jax.sharding import PartitionSpec as P

HD = 80
CAP = 2


EPS = 1e-06


def from_behind(shard, axis, by):
    length = lax.axis_size(axis)
    pairs = [(i, i + by) for i in range(length) if 0 <= i + by < length]
    return lax.ppermute(shard, axis, pairs)


def attn_kernel(heads, rows, q_ref, w_ref, b0, b1, b2, b3, b4, out_ref, att_ref):
    blocks = (b0, b1, b2, b3, b4)
    scale = HD ** (-0.5)
    width = heads * HD
    side = jnp.transpose(b0[rows:rows + 8, 0:rows].astype(jnp.float32))
    qcode = side[:, 1:2]
    order = side[:, 2:3]
    row_id = lax.broadcasted_iota(jnp.int32, (rows, rows), 0)
    col_id = lax.broadcasted_iota(jnp.int32, (rows, rows), 1)
    diag = row_id == col_id
    masks = []
    for b, blk in enumerate(blocks):
        kcode = blk[rows:rows + 1, 0:rows].astype(jnp.float32)
        m = qcode == kcode
        if b == 0:
            m = m | diag
        masks.append(m)
    for h in range(heads):
        q = q_ref[:, h * HD:(h + 1) * HD]
        scores = []
        for b, blk in enumerate(blocks):
            k = blk[0:rows, h * HD:(h + 1) * HD]
            s = lax.dot_general(q, k, (((1,), (1,)), ((), ())), preferred_element_type=jnp.float32) * scale
            scores.append(jnp.where(masks[b], s, -1e30))
        row_max = scores[0].max(axis=1, keepdims=True)
        for s in scores[1:]:
            row_max = jnp.maximum(row_max, s.max(axis=1, keepdims=True))
        exps = [jnp.exp(s - row_max) for s in scores]
        total = exps[0].sum(axis=1, keepdims=True)
        for e in exps[1:]:
            total = total + e.sum(axis=1, keepdims=True)
        acc = None
        for b, blk in enumerate(blocks):
            w = (exps[b] / total).astype(jnp.bfloat16)
            v = blk[0:rows, width + h * HD:width + (h + 1) * HD]
            p = jnp.dot(w, v, preferred_element_type=jnp.float32)
            acc = p if acc is None else acc + p
        att_ref[:, h * HD:(h + 1) * HD] = acc.astype(jnp.bfloat16)
    pick = (order == col_id.astype(jnp.float32)).astype(jnp.bfloat16)
    ordered = jnp.dot(pick, att_ref[...], preferred_element_type=jnp.float32)
    mixed = jnp.dot(ordered.astype(jnp.bfloat16), w_ref[...], preferred_element_type=jnp.float32)
    out_ref[...] = mixed.astype(out_ref.dtype)


def attention(q, w_out, blocks):
    rows, width = q.shape
    heads = width // HD
    out_width = w_out.shape[1]
    vmem = pl.BlockSpec(memory_space=pltpu.VMEM)
    flops = 2 * 2 * heads * rows * rows * len(blocks) * HD
    flops += 2 * rows * rows * width + 2 * rows * width * out_width
    return pl.pallas_call(
        functools.partial(attn_kernel, heads, rows),
        out_shape=jax.ShapeDtypeStruct((rows, out_width), jnp.bfloat16),
        in_specs=[vmem] * (2 + len(blocks)),
        out_specs=vmem,
        scratch_shapes=[pltpu.VMEM((rows, width), jnp.bfloat16)],
        cost_estimate=pl.CostEstimate(
            flops=flops,
            transcendentals=heads * rows * rows * len(blocks),
            bytes_accessed=sum(b.size * 2 for b in blocks) + q.size * 2 + w_out.size * 2 + rows * out_width * 2,
        ),
    )(q, w_out, *blocks)


def layer_norm(activations, norm_gain):
    activations = activations.astype(jnp.float32)
    row_mean = jnp.mean(activations, axis=-1, keepdims=True)
    centered = activations - row_mean
    variance = jnp.mean(centered * centered, axis=-1, keepdims=True)
    return centered * lax.rsqrt(variance + EPS) * norm_gain


def body(
    tokens,
    first_gain,
    w_query,
    w_key,
    w_value,
    w_out,
    segment_ids,
    keep_mask,
    merge_gain,
    w_merge,
    merge_index,
    destination,
):
    row_count = tokens.shape[0]
    local_width = w_query.shape[1]
    heads_here = local_width // HD
    tp_size = lax.axis_size("tp")
    seq_size = lax.axis_size("seq")
    position = lax.axis_index("tp")
    seq_index = lax.axis_index("seq")

    gathered = lax.all_to_all(
        jnp.concatenate([tokens] * tp_size, axis=1), "tp", 1, 1, tiled=True
    )

    normed = layer_norm(gathered, first_gain).astype(jnp.bfloat16)
    queries = jnp.dot(normed, w_query, preferred_element_type=jnp.float32).astype(jnp.bfloat16)
    key_rows = jnp.dot(normed, w_key, preferred_element_type=jnp.float32).astype(jnp.bfloat16)
    value_rows = jnp.dot(normed, w_value, preferred_element_type=jnp.float32).astype(jnp.bfloat16)
    code_query = segment_ids + 1
    code_key = jnp.where(keep_mask > 0, code_query, 0)
    pair_width = 2 * local_width
    local_index = merge_index - seq_index * row_count
    order = local_index.T.reshape(row_count)
    code_rows = jnp.stack([code_key, code_query, order]).astype(jnp.bfloat16)
    code_block = jnp.zeros((8, pair_width), jnp.bfloat16)
    code_block = code_block.at[0:3, :row_count].set(code_rows)
    paired = jnp.concatenate([jnp.concatenate([key_rows, value_rows], axis=1), code_block], axis=0)
    pair_list = [paired]
    for offset in (1, 2, -1, -2):
        pair_list.append(from_behind(paired, "seq", offset))
    partial_sum = attention(queries, w_out, pair_list)
    chunk = row_count // tp_size
    pieces = lax.all_to_all(partial_sum, "tp", 0, 0, tiled=True)
    mixed_sum = jnp.sum(pieces.reshape(tp_size, chunk, -1).astype(jnp.float32), axis=0)
    column = lax.dynamic_slice_in_dim(local_index, position, 1, 1)[:, 0]
    residual = jnp.take(gathered, column, axis=0)
    updated = residual.astype(jnp.float32) + mixed_sum
    picked = layer_norm(updated, merge_gain).astype(jnp.bfloat16)
    partial_proj = jnp.dot(picked, w_merge, preferred_element_type=jnp.float32)
    partial_proj = partial_proj.astype(jnp.bfloat16)
    width = partial_proj.shape[1] // tp_size
    proj_pieces = lax.all_to_all(partial_proj, "tp", 1, 0, tiled=True)
    projected = jnp.sum(proj_pieces.reshape(tp_size, chunk, width).astype(jnp.float32), axis=0)
    projected = projected.astype(jnp.bfloat16)
    slot_count = projected.shape[0]

    owner = destination // slot_count
    slot = destination - owner * slot_count
    lane = jnp.arange(slot_count)
    same_owner = owner[:, None] == owner[None, :]
    earlier = lane[None, :] < lane[:, None]
    rank = jnp.sum(jnp.where(same_owner & earlier, 1, 0), axis=1)
    send_pos = owner * CAP + rank
    target = jnp.arange(seq_size * CAP)
    send_hot = (send_pos[None, :] == target[:, None]).astype(jnp.bfloat16)
    send_rows = jnp.dot(send_hot, projected, preferred_element_type=jnp.float32)
    send_rows = send_rows.astype(jnp.bfloat16).reshape(seq_size, CAP, width)
    slot_code = (slot + 1).astype(jnp.float32)
    send_slot = jnp.dot(send_hot.astype(jnp.float32), slot_code, precision=lax.Precision.HIGHEST)
    slot_row = jnp.zeros((seq_size, 1, width), jnp.bfloat16)
    slot_row = slot_row.at[:, 0, :CAP].set(send_slot.reshape(seq_size, CAP).astype(jnp.bfloat16))
    send_buf = jnp.concatenate([send_rows, slot_row], axis=1).reshape(seq_size * (CAP + 1), width)
    recv = lax.all_to_all(send_buf, "seq", 0, 0, tiled=True).reshape(seq_size, CAP + 1, width)
    recv_rows = recv[:, :CAP, :].reshape(seq_size * CAP, width)
    recv_slot = recv[:, CAP, :CAP].reshape(seq_size * CAP).astype(jnp.int32) - 1
    recv_hot = (recv_slot[None, :] == lane[:, None]).astype(jnp.bfloat16)
    delivered = jnp.dot(recv_hot, recv_rows, preferred_element_type=jnp.float32)
    return delivered.astype(jnp.bfloat16)


def solution(mesh):
    return jax.shard_map(
        body,
        mesh=mesh,
        in_specs=(
            P("seq", "tp"),
            P(),
            P(None, "tp"),
            P(None, "tp"),
            P(None, "tp"),
            P("tp", None),
            P("seq"),
            P("seq"),
            P(),
            P("tp", None),
            P("seq", None),
            P("seq"),
        ),
        out_specs=P("seq", "tp"),
        check_vma=False,
    )
```

```python
import functools

import jax
import jax.numpy as jnp
from jax import lax
from jax.experimental import pallas as pl
from jax.experimental.pallas import tpu as pltpu
from jax.sharding import PartitionSpec as P

HD = 80
CAP = 2


EPS = 1e-06


def from_behind(shard, axis, by):
    length = lax.axis_size(axis)
    pairs = [(i, i + by) for i in range(length) if 0 <= i + by < length]
    return lax.ppermute(shard, axis, pairs)


def attn_kernel(heads, rows, span, q_ref, w_ref, b0, b1, b2, b3, out_ref, att_ref):
    blocks = ((b0, 0), (b1, 0), (b2, 0), (b3, 0), (b3, span))
    scale = HD ** (-0.5)
    width = heads * HD
    side = jnp.transpose(b0[rows:rows + 16, 0:rows].astype(jnp.float32))
    qcode = side[:, 1:2]
    order = side[:, 2:3]
    row_id = lax.broadcasted_iota(jnp.int32, (rows, rows), 0)
    col_id = lax.broadcasted_iota(jnp.int32, (rows, rows), 1)
    diag = row_id == col_id
    masks = []
    for b, (blk, at) in enumerate(blocks):
        kcode = blk[at + rows:at + rows + 1, 0:rows].astype(jnp.float32)
        m = qcode == kcode
        if b == 0:
            m = m | diag
        masks.append(m)
    for h in range(heads):
        q = q_ref[:, h * HD:(h + 1) * HD]
        scores = []
        for b, (blk, at) in enumerate(blocks):
            k = blk[at:at + rows, h * HD:(h + 1) * HD]
            s = lax.dot_general(q, k, (((1,), (1,)), ((), ())), preferred_element_type=jnp.float32) * scale
            scores.append(jnp.where(masks[b], s, -1e30))
        row_max = scores[0].max(axis=1, keepdims=True)
        for s in scores[1:]:
            row_max = jnp.maximum(row_max, s.max(axis=1, keepdims=True))
        exps = [jnp.exp(s - row_max) for s in scores]
        total = exps[0].sum(axis=1, keepdims=True)
        for e in exps[1:]:
            total = total + e.sum(axis=1, keepdims=True)
        acc = None
        for b, (blk, at) in enumerate(blocks):
            w = (exps[b] / total).astype(jnp.bfloat16)
            v = blk[at:at + rows, width + h * HD:width + (h + 1) * HD]
            p = jnp.dot(w, v, preferred_element_type=jnp.float32)
            acc = p if acc is None else acc + p
        att_ref[:, h * HD:(h + 1) * HD] = acc.astype(jnp.bfloat16)
    pick = (order == col_id.astype(jnp.float32)).astype(jnp.bfloat16)
    ordered = jnp.dot(pick, att_ref[...], preferred_element_type=jnp.float32)
    mixed = jnp.dot(ordered.astype(jnp.bfloat16), w_ref[...], preferred_element_type=jnp.float32)
    out_ref[...] = mixed.astype(out_ref.dtype)


def attention(q, w_out, blocks):
    rows, width = q.shape
    heads = width // HD
    out_width = w_out.shape[1]
    vmem = pl.BlockSpec(memory_space=pltpu.VMEM)
    span = blocks[0].shape[0]
    flops = 2 * 2 * heads * rows * rows * 5 * HD
    flops += 2 * rows * rows * width + 2 * rows * width * out_width
    return pl.pallas_call(
        functools.partial(attn_kernel, heads, rows, span),
        out_shape=jax.ShapeDtypeStruct((rows, out_width), jnp.bfloat16),
        in_specs=[vmem] * (2 + len(blocks)),
        out_specs=vmem,
        scratch_shapes=[pltpu.VMEM((rows, width), jnp.bfloat16)],
        cost_estimate=pl.CostEstimate(
            flops=flops,
            transcendentals=heads * rows * rows * 5,
            bytes_accessed=sum(b.size * 2 for b in blocks) + q.size * 2 + w_out.size * 2 + rows * out_width * 2,
        ),
    )(q, w_out, *blocks)


def layer_norm(activations, norm_gain):
    activations = activations.astype(jnp.float32)
    row_mean = jnp.mean(activations, axis=-1, keepdims=True)
    centered = activations - row_mean
    variance = jnp.mean(centered * centered, axis=-1, keepdims=True)
    return centered * lax.rsqrt(variance + EPS) * norm_gain


def body(
    tokens,
    first_gain,
    w_query,
    w_key,
    w_value,
    w_out,
    segment_ids,
    keep_mask,
    merge_gain,
    w_merge,
    merge_index,
    destination,
):
    row_count = tokens.shape[0]
    local_width = w_query.shape[1]
    heads_here = local_width // HD
    tp_size = lax.axis_size("tp")
    seq_size = lax.axis_size("seq")
    position = lax.axis_index("tp")
    seq_index = lax.axis_index("seq")

    gathered = lax.all_to_all(
        jnp.concatenate([tokens] * tp_size, axis=1), "tp", 1, 1, tiled=True
    )

    normed = layer_norm(gathered, first_gain).astype(jnp.bfloat16)
    queries = jnp.dot(normed, w_query, preferred_element_type=jnp.float32).astype(jnp.bfloat16)
    key_rows = jnp.dot(normed, w_key, preferred_element_type=jnp.float32).astype(jnp.bfloat16)
    value_rows = jnp.dot(normed, w_value, preferred_element_type=jnp.float32).astype(jnp.bfloat16)
    code_query = segment_ids + 1
    code_key = jnp.where(keep_mask > 0, code_query, 0)
    pair_width = 2 * local_width
    local_index = merge_index - seq_index * row_count
    order = local_index.T.reshape(row_count)
    code_rows = jnp.stack([code_key, code_query, order]).astype(jnp.bfloat16)
    code_block = jnp.zeros((16, pair_width), jnp.bfloat16)
    code_block = code_block.at[0:3, :row_count].set(code_rows)
    paired = jnp.concatenate([jnp.concatenate([key_rows, value_rows], axis=1), code_block], axis=0)
    from_left = from_behind(paired, "seq", 2)
    from_right = from_behind(paired, "seq", -2)
    core = seq_index % 2
    forward = jnp.where(core == 0, from_right, from_left)
    swap_pairs = [(i, i ^ 1) for i in range(seq_size)]
    swapped = lax.ppermute(jnp.concatenate([paired, forward], axis=0), "seq", swap_pairs)
    pair_list = [paired, from_left, from_right, swapped]
    partial_sum = attention(queries, w_out, pair_list)
    chunk = row_count // tp_size
    pieces = lax.all_to_all(partial_sum, "tp", 0, 0, tiled=True)
    mixed_sum = jnp.sum(pieces.reshape(tp_size, chunk, -1).astype(jnp.float32), axis=0)
    column = lax.dynamic_slice_in_dim(local_index, position, 1, 1)[:, 0]
    residual = jnp.take(gathered, column, axis=0)
    updated = residual.astype(jnp.float32) + mixed_sum
    picked = layer_norm(updated, merge_gain).astype(jnp.bfloat16)
    partial_proj = jnp.dot(picked, w_merge, preferred_element_type=jnp.float32)
    partial_proj = partial_proj.astype(jnp.bfloat16)
    width = partial_proj.shape[1] // tp_size
    proj_pieces = lax.all_to_all(partial_proj, "tp", 1, 0, tiled=True)
    projected = jnp.sum(proj_pieces.reshape(tp_size, chunk, width).astype(jnp.float32), axis=0)
    projected = projected.astype(jnp.bfloat16)
    slot_count = projected.shape[0]

    owner = destination // slot_count
    slot = destination - owner * slot_count
    lane = jnp.arange(slot_count)
    same_owner = owner[:, None] == owner[None, :]
    earlier = lane[None, :] < lane[:, None]
    rank = jnp.sum(jnp.where(same_owner & earlier, 1, 0), axis=1)
    send_pos = owner * CAP + rank
    target = jnp.arange(seq_size * CAP)
    send_hot = (send_pos[None, :] == target[:, None]).astype(jnp.bfloat16)
    send_rows = jnp.dot(send_hot, projected, preferred_element_type=jnp.float32)
    send_rows = send_rows.astype(jnp.bfloat16).reshape(seq_size, CAP, width)
    slot_code = (slot + 1).astype(jnp.float32)
    send_slot = jnp.dot(send_hot.astype(jnp.float32), slot_code, precision=lax.Precision.HIGHEST)
    slot_row = jnp.zeros((seq_size, 1, width), jnp.bfloat16)
    slot_row = slot_row.at[:, 0, :CAP].set(send_slot.reshape(seq_size, CAP).astype(jnp.bfloat16))
    send_buf = jnp.concatenate([send_rows, slot_row], axis=1).reshape(seq_size * (CAP + 1), width)
    recv = lax.all_to_all(send_buf, "seq", 0, 0, tiled=True).reshape(seq_size, CAP + 1, width)
    recv_rows = recv[:, :CAP, :].reshape(seq_size * CAP, width)
    recv_slot = recv[:, CAP, :CAP].reshape(seq_size * CAP).astype(jnp.int32) - 1
    recv_hot = (recv_slot[None, :] == lane[:, None]).astype(jnp.bfloat16)
    delivered = jnp.dot(recv_hot, recv_rows, preferred_element_type=jnp.float32)
    return delivered.astype(jnp.bfloat16)


def solution(mesh):
    return jax.shard_map(
        body,
        mesh=mesh,
        in_specs=(
            P("seq", "tp"),
            P(),
            P(None, "tp"),
            P(None, "tp"),
            P(None, "tp"),
            P("tp", None),
            P("seq"),
            P("seq"),
            P(),
            P("tp", None),
            P("seq", None),
            P("seq"),
        ),
        out_specs=P("seq", "tp"),
        check_vma=False,
    )
```

```python
import functools

import jax
import jax.numpy as jnp
from jax import lax
from jax.experimental import pallas as pl
from jax.experimental.pallas import tpu as pltpu
from jax.sharding import PartitionSpec as P

HD = 80
CAP = 2


EPS = 1e-06


def from_behind(shard, axis, by):
    length = lax.axis_size(axis)
    pairs = [(i, i + by) for i in range(length) if 0 <= i + by < length]
    return lax.ppermute(shard, axis, pairs)


def attn_kernel(heads, rows, q_ref, w_ref, b0, b1, b2, b3, b4, out_ref, att_ref):
    blocks = (b0, b1, b2, b3, b4)
    scale = HD ** (-0.5)
    width = heads * HD
    side = jnp.transpose(b0[rows:rows + 8, 0:rows].astype(jnp.float32))
    qcode = side[:, 1:2]
    order = side[:, 2:3]
    row_id = lax.broadcasted_iota(jnp.int32, (rows, rows), 0)
    col_id = lax.broadcasted_iota(jnp.int32, (rows, rows), 1)
    diag = row_id == col_id
    masks = []
    for b, blk in enumerate(blocks):
        kcode = blk[rows:rows + 1, 0:rows].astype(jnp.float32)
        m = qcode == kcode
        if b == 0:
            m = m | diag
        masks.append(m)
    for h in range(heads):
        q = q_ref[:, h * HD:(h + 1) * HD]
        scores = []
        for b, blk in enumerate(blocks):
            k = blk[0:rows, h * HD:(h + 1) * HD]
            s = lax.dot_general(q, k, (((1,), (1,)), ((), ())), preferred_element_type=jnp.float32) * scale
            scores.append(jnp.where(masks[b], s, -1e30))
        row_max = scores[0].max(axis=1, keepdims=True)
        for s in scores[1:]:
            row_max = jnp.maximum(row_max, s.max(axis=1, keepdims=True))
        exps = [jnp.exp(s - row_max) for s in scores]
        total = exps[0].sum(axis=1, keepdims=True)
        for e in exps[1:]:
            total = total + e.sum(axis=1, keepdims=True)
        acc = None
        for b, blk in enumerate(blocks):
            w = (exps[b] / total).astype(jnp.bfloat16)
            v = blk[0:rows, width + h * HD:width + (h + 1) * HD]
            p = jnp.dot(w, v, preferred_element_type=jnp.float32)
            acc = p if acc is None else acc + p
        att_ref[:, h * HD:(h + 1) * HD] = acc.astype(jnp.bfloat16)
    pick = (order == col_id.astype(jnp.float32)).astype(jnp.bfloat16)
    ordered = jnp.dot(pick, att_ref[...], preferred_element_type=jnp.float32)
    mixed = jnp.dot(ordered.astype(jnp.bfloat16), w_ref[...], preferred_element_type=jnp.float32)
    out_ref[...] = mixed.astype(out_ref.dtype)


def attention(q, w_out, blocks):
    rows, width = q.shape
    heads = width // HD
    out_width = w_out.shape[1]
    vmem = pl.BlockSpec(memory_space=pltpu.VMEM)
    flops = 2 * 2 * heads * rows * rows * len(blocks) * HD
    flops += 2 * rows * rows * width + 2 * rows * width * out_width
    return pl.pallas_call(
        functools.partial(attn_kernel, heads, rows),
        out_shape=jax.ShapeDtypeStruct((rows, out_width), jnp.bfloat16),
        in_specs=[vmem] * (2 + len(blocks)),
        out_specs=vmem,
        scratch_shapes=[pltpu.VMEM((rows, width), jnp.bfloat16)],
        cost_estimate=pl.CostEstimate(
            flops=flops,
            transcendentals=heads * rows * rows * len(blocks),
            bytes_accessed=sum(b.size * 2 for b in blocks) + q.size * 2 + w_out.size * 2 + rows * out_width * 2,
        ),
    )(q, w_out, *blocks)


def layer_norm(activations, norm_gain):
    activations = activations.astype(jnp.float32)
    row_mean = jnp.mean(activations, axis=-1, keepdims=True)
    centered = activations - row_mean
    variance = jnp.mean(centered * centered, axis=-1, keepdims=True)
    return centered * lax.rsqrt(variance + EPS) * norm_gain


def body(
    tokens,
    first_gain,
    w_query,
    w_key,
    w_value,
    w_out,
    segment_ids,
    keep_mask,
    merge_gain,
    w_merge,
    merge_index,
    destination,
):
    row_count = tokens.shape[0]
    local_width = w_query.shape[1]
    heads_here = local_width // HD
    tp_size = lax.axis_size("tp")
    seq_size = lax.axis_size("seq")
    position = lax.axis_index("tp")
    seq_index = lax.axis_index("seq")

    gathered = lax.all_gather(tokens, "tp", axis=1, tiled=True)

    normed = layer_norm(gathered, first_gain).astype(jnp.bfloat16)
    queries = jnp.dot(normed, w_query, preferred_element_type=jnp.float32).astype(jnp.bfloat16)
    key_rows = jnp.dot(normed, w_key, preferred_element_type=jnp.float32).astype(jnp.bfloat16)
    value_rows = jnp.dot(normed, w_value, preferred_element_type=jnp.float32).astype(jnp.bfloat16)
    code_query = segment_ids + 1
    code_key = jnp.where(keep_mask > 0, code_query, 0)
    pair_width = 2 * local_width
    local_index = merge_index - seq_index * row_count
    order = local_index.T.reshape(row_count)
    code_rows = jnp.stack([code_key, code_query, order]).astype(jnp.bfloat16)
    code_block = jnp.zeros((8, pair_width), jnp.bfloat16)
    code_block = code_block.at[0:3, :row_count].set(code_rows)
    paired = jnp.concatenate([jnp.concatenate([key_rows, value_rows], axis=1), code_block], axis=0)
    pair_list = [paired]
    for offset in (1, 2, -1, -2):
        pair_list.append(from_behind(paired, "seq", offset))
    partial_sum = attention(queries, w_out, pair_list)
    chunk = row_count // tp_size
    pieces = lax.all_to_all(partial_sum, "tp", 0, 0, tiled=True)
    mixed_sum = jnp.sum(pieces.reshape(tp_size, chunk, -1).astype(jnp.float32), axis=0)
    column = lax.dynamic_slice_in_dim(local_index, position, 1, 1)[:, 0]
    residual = jnp.take(gathered, column, axis=0)
    updated = residual.astype(jnp.float32) + mixed_sum
    picked = layer_norm(updated, merge_gain).astype(jnp.bfloat16)
    partial_proj = jnp.dot(picked, w_merge, preferred_element_type=jnp.float32)
    partial_proj = partial_proj.astype(jnp.bfloat16)
    width = partial_proj.shape[1] // tp_size
    proj_pieces = lax.all_to_all(partial_proj, "tp", 1, 0, tiled=True)
    projected = jnp.sum(proj_pieces.reshape(tp_size, chunk, width).astype(jnp.float32), axis=0)
    projected = projected.astype(jnp.bfloat16)
    slot_count = projected.shape[0]

    owner = destination // slot_count
    slot = destination - owner * slot_count
    lane = jnp.arange(slot_count)
    same_owner = owner[:, None] == owner[None, :]
    earlier = lane[None, :] < lane[:, None]
    rank = jnp.sum(jnp.where(same_owner & earlier, 1, 0), axis=1)
    send_pos = owner * CAP + rank
    target = jnp.arange(seq_size * CAP)
    send_hot = (send_pos[None, :] == target[:, None]).astype(jnp.bfloat16)
    send_rows = jnp.dot(send_hot, projected, preferred_element_type=jnp.float32)
    send_rows = send_rows.astype(jnp.bfloat16).reshape(seq_size, CAP, width)
    slot_code = (slot + 1).astype(jnp.float32)
    send_slot = jnp.dot(send_hot.astype(jnp.float32), slot_code, precision=lax.Precision.HIGHEST)
    slot_row = jnp.zeros((seq_size, 1, width), jnp.bfloat16)
    slot_row = slot_row.at[:, 0, :CAP].set(send_slot.reshape(seq_size, CAP).astype(jnp.bfloat16))
    send_buf = jnp.concatenate([send_rows, slot_row], axis=1).reshape(seq_size * (CAP + 1), width)
    recv = lax.all_to_all(send_buf, "seq", 0, 0, tiled=True).reshape(seq_size, CAP + 1, width)
    recv_rows = recv[:, :CAP, :].reshape(seq_size * CAP, width)
    recv_slot = recv[:, CAP, :CAP].reshape(seq_size * CAP).astype(jnp.int32) - 1
    recv_hot = (recv_slot[None, :] == lane[:, None]).astype(jnp.bfloat16)
    delivered = jnp.dot(recv_hot, recv_rows, preferred_element_type=jnp.float32)
    return delivered.astype(jnp.bfloat16)


def solution(mesh):
    return jax.shard_map(
        body,
        mesh=mesh,
        in_specs=(
            P("seq", "tp"),
            P(),
            P(None, "tp"),
            P(None, "tp"),
            P(None, "tp"),
            P("tp", None),
            P("seq"),
            P("seq"),
            P(),
            P("tp", None),
            P("seq", None),
            P("seq"),
        ),
        out_specs=P("seq", "tp"),
        check_vma=False,
    )
```

```python
import functools

import jax
import jax.numpy as jnp
from jax import lax
from jax.experimental import pallas as pl
from jax.experimental.pallas import tpu as pltpu
from jax.sharding import PartitionSpec as P

HD = 80
CAP = 2


EPS = 1e-06


def from_behind(shard, axis, by):
    length = lax.axis_size(axis)
    pairs = [(i, i + by) for i in range(length) if 0 <= i + by < length]
    return lax.ppermute(shard, axis, pairs)


def attn_kernel(heads, rows, q_hbm, w_hbm, b0, b1, b2, b3, b4, out_ref,
                q_ref, w_ref, blk_ref, score_ref, att_ref, sems):
    sources = (b0, b1, b2, b3, b4)
    nblk = len(sources)
    scale = HD ** (-0.5)
    width = heads * HD
    copies = [pltpu.make_async_copy(sources[0], blk_ref.at[0], sems.at[0]),
              pltpu.make_async_copy(q_hbm, q_ref, sems.at[nblk])]
    copies += [pltpu.make_async_copy(sources[b], blk_ref.at[b], sems.at[b]) for b in range(1, nblk)]
    copies.append(pltpu.make_async_copy(w_hbm, w_ref, sems.at[nblk + 1]))
    for c in copies:
        c.start()
    copies[0].wait()
    copies[1].wait()
    side = jnp.transpose(blk_ref[0, rows:rows + 8, 0:rows].astype(jnp.float32))
    qcode = side[:, 1:2]
    order = side[:, 2:3]
    row_id = lax.broadcasted_iota(jnp.int32, (rows, rows), 0)
    col_id = lax.broadcasted_iota(jnp.int32, (rows, rows), 1)
    diag = row_id == col_id
    row_max = [None] * heads
    for b in range(nblk):
        if b >= 1:
            copies[b + 1].wait()
        kcode = blk_ref[b, rows:rows + 1, 0:rows].astype(jnp.float32)
        mask = qcode == kcode
        if b == 0:
            mask = mask | diag
        for h in range(heads):
            q = q_ref[:, h * HD:(h + 1) * HD]
            k = blk_ref[b, 0:rows, h * HD:(h + 1) * HD]
            s = lax.dot_general(q, k, (((1,), (1,)), ((), ())), preferred_element_type=jnp.float32) * scale
            s = jnp.where(mask, s, -1e30)
            score_ref[h * nblk + b] = s
            m = s.max(axis=1, keepdims=True)
            row_max[h] = m if row_max[h] is None else jnp.maximum(row_max[h], m)
    for h in range(heads):
        exps = [jnp.exp(score_ref[h * nblk + b] - row_max[h]) for b in range(nblk)]
        total = exps[0].sum(axis=1, keepdims=True)
        for e in exps[1:]:
            total = total + e.sum(axis=1, keepdims=True)
        acc = None
        for b in range(nblk):
            w = (exps[b] / total).astype(jnp.bfloat16)
            v = blk_ref[b, 0:rows, width + h * HD:width + (h + 1) * HD]
            p = jnp.dot(w, v, preferred_element_type=jnp.float32)
            acc = p if acc is None else acc + p
        att_ref[:, h * HD:(h + 1) * HD] = acc.astype(jnp.bfloat16)
    pick = (order == col_id.astype(jnp.float32)).astype(jnp.bfloat16)
    ordered = jnp.dot(pick, att_ref[...], preferred_element_type=jnp.float32)
    copies[-1].wait()
    mixed = jnp.dot(ordered.astype(jnp.bfloat16), w_ref[...], preferred_element_type=jnp.float32)
    out_ref[...] = mixed.astype(out_ref.dtype)


def attention(q, w_out, blocks):
    rows, width = q.shape
    heads = width // HD
    out_width = w_out.shape[1]
    nblk = len(blocks)
    anywhere = pl.BlockSpec(memory_space=pl.ANY)
    flops = 2 * 2 * heads * rows * rows * nblk * HD
    flops += 2 * rows * rows * width + 2 * rows * width * out_width
    return pl.pallas_call(
        functools.partial(attn_kernel, heads, rows),
        out_shape=jax.ShapeDtypeStruct((rows, out_width), jnp.bfloat16),
        in_specs=[anywhere] * (2 + nblk),
        out_specs=pl.BlockSpec(memory_space=pltpu.VMEM),
        scratch_shapes=[
            pltpu.VMEM(q.shape, jnp.bfloat16),
            pltpu.VMEM(w_out.shape, jnp.bfloat16),
            pltpu.VMEM((nblk,) + blocks[0].shape, jnp.bfloat16),
            pltpu.VMEM((heads * nblk, rows, rows), jnp.float32),
            pltpu.VMEM((rows, width), jnp.bfloat16),
            pltpu.SemaphoreType.DMA((nblk + 2,)),
        ],
        cost_estimate=pl.CostEstimate(
            flops=flops,
            transcendentals=heads * rows * rows * nblk,
            bytes_accessed=sum(b.size * 2 for b in blocks) + q.size * 2 + w_out.size * 2 + rows * out_width * 2,
        ),
    )(q, w_out, *blocks)


def layer_norm(activations, norm_gain):
    activations = activations.astype(jnp.float32)
    row_mean = jnp.mean(activations, axis=-1, keepdims=True)
    centered = activations - row_mean
    variance = jnp.mean(centered * centered, axis=-1, keepdims=True)
    return centered * lax.rsqrt(variance + EPS) * norm_gain


def body(
    tokens,
    first_gain,
    w_query,
    w_key,
    w_value,
    w_out,
    segment_ids,
    keep_mask,
    merge_gain,
    w_merge,
    merge_index,
    destination,
):
    row_count = tokens.shape[0]
    local_width = w_query.shape[1]
    heads_here = local_width // HD
    tp_size = lax.axis_size("tp")
    seq_size = lax.axis_size("seq")
    position = lax.axis_index("tp")
    seq_index = lax.axis_index("seq")

    gathered = lax.all_gather(tokens, "tp", axis=1, tiled=True)

    normed = layer_norm(gathered, first_gain).astype(jnp.bfloat16)
    queries = jnp.dot(normed, w_query, preferred_element_type=jnp.float32).astype(jnp.bfloat16)
    key_rows = jnp.dot(normed, w_key, preferred_element_type=jnp.float32).astype(jnp.bfloat16)
    value_rows = jnp.dot(normed, w_value, preferred_element_type=jnp.float32).astype(jnp.bfloat16)
    code_query = segment_ids + 1
    code_key = jnp.where(keep_mask > 0, code_query, 0)
    pair_width = 2 * local_width
    local_index = merge_index - seq_index * row_count
    order = local_index.T.reshape(row_count)
    code_rows = jnp.stack([code_key, code_query, order]).astype(jnp.bfloat16)
    code_block = jnp.zeros((8, pair_width), jnp.bfloat16)
    code_block = code_block.at[0:3, :row_count].set(code_rows)
    paired = jnp.concatenate([jnp.concatenate([key_rows, value_rows], axis=1), code_block], axis=0)
    pair_list = [paired]
    for offset in (1, 2, -1, -2):
        pair_list.append(from_behind(paired, "seq", offset))
    partial_sum = attention(queries, w_out, pair_list)
    chunk = row_count // tp_size
    pieces = lax.all_to_all(partial_sum, "tp", 0, 0, tiled=True)
    mixed_sum = jnp.sum(pieces.reshape(tp_size, chunk, -1).astype(jnp.float32), axis=0)
    column = lax.dynamic_slice_in_dim(local_index, position, 1, 1)[:, 0]
    residual = jnp.take(gathered, column, axis=0)
    updated = residual.astype(jnp.float32) + mixed_sum
    picked = layer_norm(updated, merge_gain).astype(jnp.bfloat16)
    partial_proj = jnp.dot(picked, w_merge, preferred_element_type=jnp.float32)
    partial_proj = partial_proj.astype(jnp.bfloat16)
    width = partial_proj.shape[1] // tp_size
    proj_pieces = lax.all_to_all(partial_proj, "tp", 1, 0, tiled=True)
    projected = jnp.sum(proj_pieces.reshape(tp_size, chunk, width).astype(jnp.float32), axis=0)
    projected = projected.astype(jnp.bfloat16)
    slot_count = projected.shape[0]

    owner = destination // slot_count
    slot = destination - owner * slot_count
    lane = jnp.arange(slot_count)
    same_owner = owner[:, None] == owner[None, :]
    earlier = lane[None, :] < lane[:, None]
    rank = jnp.sum(jnp.where(same_owner & earlier, 1, 0), axis=1)
    send_pos = owner * CAP + rank
    target = jnp.arange(seq_size * CAP)
    send_hot = (send_pos[None, :] == target[:, None]).astype(jnp.bfloat16)
    send_rows = jnp.dot(send_hot, projected, preferred_element_type=jnp.float32)
    send_rows = send_rows.astype(jnp.bfloat16).reshape(seq_size, CAP, width)
    slot_code = (slot + 1).astype(jnp.float32)
    send_slot = jnp.dot(send_hot.astype(jnp.float32), slot_code, precision=lax.Precision.HIGHEST)
    slot_row = jnp.zeros((seq_size, 1, width), jnp.bfloat16)
    slot_row = slot_row.at[:, 0, :CAP].set(send_slot.reshape(seq_size, CAP).astype(jnp.bfloat16))
    send_buf = jnp.concatenate([send_rows, slot_row], axis=1).reshape(seq_size * (CAP + 1), width)
    recv = lax.all_to_all(send_buf, "seq", 0, 0, tiled=True).reshape(seq_size, CAP + 1, width)
    recv_rows = recv[:, :CAP, :].reshape(seq_size * CAP, width)
    recv_slot = recv[:, CAP, :CAP].reshape(seq_size * CAP).astype(jnp.int32) - 1
    recv_hot = (recv_slot[None, :] == lane[:, None]).astype(jnp.bfloat16)
    delivered = jnp.dot(recv_hot, recv_rows, preferred_element_type=jnp.float32)
    return delivered.astype(jnp.bfloat16)


def solution(mesh):
    return jax.shard_map(
        body,
        mesh=mesh,
        in_specs=(
            P("seq", "tp"),
            P(),
            P(None, "tp"),
            P(None, "tp"),
            P(None, "tp"),
            P("tp", None),
            P("seq"),
            P("seq"),
            P(),
            P("tp", None),
            P("seq", None),
            P("seq"),
        ),
        out_specs=P("seq", "tp"),
        check_vma=False,
    )
```

```python
import functools

import jax
import jax.numpy as jnp
from jax import lax
from jax.experimental import pallas as pl
from jax.experimental.pallas import tpu as pltpu
from jax.sharding import PartitionSpec as P

HD = 80
CAP = 2


EPS = 1e-06


def from_behind(shard, axis, by):
    length = lax.axis_size(axis)
    pairs = [(i, i + by) for i in range(length) if 0 <= i + by < length]
    return lax.ppermute(shard, axis, pairs)


def attn_kernel(heads, rows, q_hbm, w_hbm, b0, b1, b2, b3, b4, out_ref,
                q_ref, w_ref, blk_ref, score_ref, att_ref, sems):
    sources = (b0, b1, b2, b3, b4)
    nblk = len(sources)
    scale = HD ** (-0.5)
    width = heads * HD
    copies = [pltpu.make_async_copy(sources[0], blk_ref.at[0], sems.at[0]),
              pltpu.make_async_copy(q_hbm, q_ref, sems.at[nblk])]
    copies += [pltpu.make_async_copy(sources[b], blk_ref.at[b], sems.at[b]) for b in range(1, nblk)]
    copies.append(pltpu.make_async_copy(w_hbm, w_ref, sems.at[nblk + 1]))
    for c in copies:
        c.start()
    copies[0].wait()
    copies[1].wait()
    side = jnp.transpose(blk_ref[0, rows:rows + 8, 0:rows].astype(jnp.float32))
    qcode = side[:, 1:2]
    order = side[:, 2:3]
    row_id = lax.broadcasted_iota(jnp.int32, (rows, rows), 0)
    col_id = lax.broadcasted_iota(jnp.int32, (rows, rows), 1)
    diag = row_id == col_id
    row_max = [None] * heads
    for b in range(nblk):
        if b >= 1:
            copies[b + 1].wait()
        kcode = blk_ref[b, rows:rows + 1, 0:rows].astype(jnp.float32)
        mask = qcode == kcode
        if b == 0:
            mask = mask | diag
        for h in range(heads):
            q = q_ref[:, h * HD:(h + 1) * HD]
            k = blk_ref[b, 0:rows, h * HD:(h + 1) * HD]
            s = lax.dot_general(q, k, (((1,), (1,)), ((), ())), preferred_element_type=jnp.float32) * scale
            s = jnp.where(mask, s, -1e30)
            score_ref[h * nblk + b] = s
            m = s.max(axis=1, keepdims=True)
            row_max[h] = m if row_max[h] is None else jnp.maximum(row_max[h], m)
    for h in range(heads):
        exps = [jnp.exp(score_ref[h * nblk + b] - row_max[h]) for b in range(nblk)]
        total = exps[0].sum(axis=1, keepdims=True)
        for e in exps[1:]:
            total = total + e.sum(axis=1, keepdims=True)
        acc = None
        for b in range(nblk):
            w = (exps[b] / total).astype(jnp.bfloat16)
            v = blk_ref[b, 0:rows, width + h * HD:width + (h + 1) * HD]
            p = jnp.dot(w, v, preferred_element_type=jnp.float32)
            acc = p if acc is None else acc + p
        att_ref[:, h * HD:(h + 1) * HD] = acc.astype(jnp.bfloat16)
    pick = (order == col_id.astype(jnp.float32)).astype(jnp.bfloat16)
    ordered = jnp.dot(pick, att_ref[...], preferred_element_type=jnp.float32)
    copies[-1].wait()
    mixed = jnp.dot(ordered.astype(jnp.bfloat16), w_ref[...], preferred_element_type=jnp.float32)
    out_ref[...] = mixed.astype(out_ref.dtype)


def attention(q, w_out, blocks):
    rows, width = q.shape
    heads = width // HD
    out_width = w_out.shape[1]
    nblk = len(blocks)
    anywhere = pl.BlockSpec(memory_space=pl.ANY)
    flops = 2 * 2 * heads * rows * rows * nblk * HD
    flops += 2 * rows * rows * width + 2 * rows * width * out_width
    return pl.pallas_call(
        functools.partial(attn_kernel, heads, rows),
        out_shape=jax.ShapeDtypeStruct((rows, out_width), jnp.bfloat16),
        in_specs=[anywhere] * (2 + nblk),
        out_specs=pl.BlockSpec(memory_space=pltpu.VMEM),
        scratch_shapes=[
            pltpu.VMEM(q.shape, jnp.bfloat16),
            pltpu.VMEM(w_out.shape, jnp.bfloat16),
            pltpu.VMEM((nblk,) + blocks[0].shape, jnp.bfloat16),
            pltpu.VMEM((heads * nblk, rows, rows), jnp.float32),
            pltpu.VMEM((rows, width), jnp.bfloat16),
            pltpu.SemaphoreType.DMA((nblk + 2,)),
        ],
        cost_estimate=pl.CostEstimate(
            flops=flops,
            transcendentals=heads * rows * rows * nblk,
            bytes_accessed=sum(b.size * 2 for b in blocks) + q.size * 2 + w_out.size * 2 + rows * out_width * 2,
        ),
    )(q, w_out, *blocks)


def layer_norm(activations, norm_gain):
    activations = activations.astype(jnp.float32)
    row_mean = jnp.mean(activations, axis=-1, keepdims=True)
    centered = activations - row_mean
    variance = jnp.mean(centered * centered, axis=-1, keepdims=True)
    return centered * lax.rsqrt(variance + EPS) * norm_gain


def body(
    tokens,
    first_gain,
    w_query,
    w_key,
    w_value,
    w_out,
    segment_ids,
    keep_mask,
    merge_gain,
    w_merge,
    merge_index,
    destination,
):
    row_count = tokens.shape[0]
    local_width = w_query.shape[1]
    heads_here = local_width // HD
    tp_size = lax.axis_size("tp")
    seq_size = lax.axis_size("seq")
    position = lax.axis_index("tp")
    seq_index = lax.axis_index("seq")

    gathered = lax.all_gather(tokens, "tp", axis=1, tiled=True)

    normed = layer_norm(gathered, first_gain).astype(jnp.bfloat16)
    queries = jnp.dot(normed, w_query, preferred_element_type=jnp.float32).astype(jnp.bfloat16)
    key_rows = jnp.dot(normed, w_key, preferred_element_type=jnp.float32).astype(jnp.bfloat16)
    value_rows = jnp.dot(normed, w_value, preferred_element_type=jnp.float32).astype(jnp.bfloat16)
    code_query = segment_ids + 1
    code_key = jnp.where(keep_mask > 0, code_query, 0)
    pair_width = 2 * local_width
    local_index = merge_index - seq_index * row_count
    order = local_index.T.reshape(row_count)
    code_rows = jnp.stack([code_key, code_query, order]).astype(jnp.bfloat16)
    code_block = jnp.zeros((8, pair_width), jnp.bfloat16)
    code_block = code_block.at[0:3, :row_count].set(code_rows)
    paired = jnp.concatenate([jnp.concatenate([key_rows, value_rows], axis=1), code_block], axis=0)
    pair_list = [paired]
    for offset in (1, 2, -1, -2):
        pair_list.append(from_behind(paired, "seq", offset))
    partial_sum = attention(queries, w_out, pair_list)
    chunk = row_count // tp_size
    pieces = lax.all_to_all(partial_sum, "tp", 0, 0, tiled=True)
    mixed_sum = jnp.sum(pieces.reshape(tp_size, chunk, -1).astype(jnp.float32), axis=0)
    column = lax.dynamic_slice_in_dim(local_index, position, 1, 1)[:, 0]
    residual = jnp.take(gathered, column, axis=0)
    updated = residual.astype(jnp.float32) + mixed_sum
    picked = layer_norm(updated, merge_gain).astype(jnp.bfloat16)
    partial_proj = jnp.dot(picked, w_merge, preferred_element_type=jnp.float32)
    partial_proj = partial_proj.astype(jnp.bfloat16)
    width = partial_proj.shape[1] // tp_size
    proj_all = lax.all_gather(partial_proj, "tp", axis=0, tiled=False)
    proj_pieces = lax.dynamic_slice_in_dim(proj_all, position * width, width, 2)
    projected = jnp.sum(proj_pieces.astype(jnp.float32), axis=0)
    projected = projected.astype(jnp.bfloat16)
    slot_count = projected.shape[0]

    owner = destination // slot_count
    slot = destination - owner * slot_count
    lane = jnp.arange(slot_count)
    same_owner = owner[:, None] == owner[None, :]
    earlier = lane[None, :] < lane[:, None]
    rank = jnp.sum(jnp.where(same_owner & earlier, 1, 0), axis=1)
    send_pos = owner * CAP + rank
    target = jnp.arange(seq_size * CAP)
    send_hot = (send_pos[None, :] == target[:, None]).astype(jnp.bfloat16)
    send_rows = jnp.dot(send_hot, projected, preferred_element_type=jnp.float32)
    send_rows = send_rows.astype(jnp.bfloat16).reshape(seq_size, CAP, width)
    slot_code = (slot + 1).astype(jnp.float32)
    send_slot = jnp.dot(send_hot.astype(jnp.float32), slot_code, precision=lax.Precision.HIGHEST)
    slot_row = jnp.zeros((seq_size, 1, width), jnp.bfloat16)
    slot_row = slot_row.at[:, 0, :CAP].set(send_slot.reshape(seq_size, CAP).astype(jnp.bfloat16))
    send_buf = jnp.concatenate([send_rows, slot_row], axis=1).reshape(seq_size * (CAP + 1), width)
    recv = lax.all_to_all(send_buf, "seq", 0, 0, tiled=True).reshape(seq_size, CAP + 1, width)
    recv_rows = recv[:, :CAP, :].reshape(seq_size * CAP, width)
    recv_slot = recv[:, CAP, :CAP].reshape(seq_size * CAP).astype(jnp.int32) - 1
    recv_hot = (recv_slot[None, :] == lane[:, None]).astype(jnp.bfloat16)
    delivered = jnp.dot(recv_hot, recv_rows, preferred_element_type=jnp.float32)
    return delivered.astype(jnp.bfloat16)


def solution(mesh):
    return jax.shard_map(
        body,
        mesh=mesh,
        in_specs=(
            P("seq", "tp"),
            P(),
            P(None, "tp"),
            P(None, "tp"),
            P(None, "tp"),
            P("tp", None),
            P("seq"),
            P("seq"),
            P(),
            P("tp", None),
            P("seq", None),
            P("seq"),
        ),
        out_specs=P("seq", "tp"),
        check_vma=False,
    )
```

```python
import functools

import jax
import jax.numpy as jnp
from jax import lax
from jax.experimental import pallas as pl
from jax.experimental.pallas import tpu as pltpu
from jax.sharding import PartitionSpec as P

HD = 80
CAP = 2


EPS = 1e-06


def from_behind(shard, axis, by):
    length = lax.axis_size(axis)
    pairs = [(i, i + by) for i in range(length) if 0 <= i + by < length]
    return lax.ppermute(shard, axis, pairs)


def attn_kernel(heads, rows, q_hbm, w_hbm, b0, b1, b2, b3, b4, out_ref,
                q_ref, w_ref, blk_ref, score_ref, att_ref, sems):
    sources = (b0, b1, b2, b3, b4)
    nblk = len(sources)
    scale = HD ** (-0.5)
    width = heads * HD
    copies = [pltpu.make_async_copy(sources[0], blk_ref.at[0], sems.at[0]),
              pltpu.make_async_copy(q_hbm, q_ref, sems.at[nblk])]
    copies += [pltpu.make_async_copy(sources[b], blk_ref.at[b], sems.at[b]) for b in range(1, nblk)]
    copies.append(pltpu.make_async_copy(w_hbm, w_ref, sems.at[nblk + 1]))
    for c in copies:
        c.start()
    copies[0].wait()
    copies[1].wait()
    side = jnp.transpose(blk_ref[0, rows:rows + 8, 0:rows].astype(jnp.float32))
    qcode = side[:, 1:2]
    order = side[:, 2:3]
    row_id = lax.broadcasted_iota(jnp.int32, (rows, rows), 0)
    col_id = lax.broadcasted_iota(jnp.int32, (rows, rows), 1)
    diag = row_id == col_id
    row_max = [None] * heads
    for b in range(nblk):
        if b >= 1:
            copies[b + 1].wait()
        kcode = blk_ref[b, rows:rows + 1, 0:rows].astype(jnp.float32)
        mask = qcode == kcode
        if b == 0:
            mask = mask | diag
        for h in range(heads):
            q = q_ref[:, h * HD:(h + 1) * HD]
            k = blk_ref[b, 0:rows, h * HD:(h + 1) * HD]
            s = lax.dot_general(q, k, (((1,), (1,)), ((), ())), preferred_element_type=jnp.float32) * scale
            s = jnp.where(mask, s, -1e30)
            score_ref[h * nblk + b] = s
            m = s.max(axis=1, keepdims=True)
            row_max[h] = m if row_max[h] is None else jnp.maximum(row_max[h], m)
    for h in range(heads):
        exps = [jnp.exp(score_ref[h * nblk + b] - row_max[h]) for b in range(nblk)]
        total = exps[0].sum(axis=1, keepdims=True)
        for e in exps[1:]:
            total = total + e.sum(axis=1, keepdims=True)
        acc = None
        for b in range(nblk):
            w = (exps[b] / total).astype(jnp.bfloat16)
            v = blk_ref[b, 0:rows, width + h * HD:width + (h + 1) * HD]
            p = jnp.dot(w, v, preferred_element_type=jnp.float32)
            acc = p if acc is None else acc + p
        att_ref[:, h * HD:(h + 1) * HD] = acc.astype(jnp.bfloat16)
    pick = (order == col_id.astype(jnp.float32)).astype(jnp.bfloat16)
    ordered = jnp.dot(pick, att_ref[...], preferred_element_type=jnp.float32)
    copies[-1].wait()
    mixed = jnp.dot(ordered.astype(jnp.bfloat16), w_ref[...], preferred_element_type=jnp.float32)
    out_ref[...] = mixed.astype(out_ref.dtype)


def attention(q, w_out, blocks):
    rows, width = q.shape
    heads = width // HD
    out_width = w_out.shape[1]
    nblk = len(blocks)
    anywhere = pl.BlockSpec(memory_space=pl.ANY)
    flops = 2 * 2 * heads * rows * rows * nblk * HD
    flops += 2 * rows * rows * width + 2 * rows * width * out_width
    return pl.pallas_call(
        functools.partial(attn_kernel, heads, rows),
        out_shape=jax.ShapeDtypeStruct((rows, out_width), jnp.bfloat16),
        in_specs=[anywhere] * (2 + nblk),
        out_specs=pl.BlockSpec(memory_space=pltpu.VMEM),
        scratch_shapes=[
            pltpu.VMEM(q.shape, jnp.bfloat16),
            pltpu.VMEM(w_out.shape, jnp.bfloat16),
            pltpu.VMEM((nblk,) + blocks[0].shape, jnp.bfloat16),
            pltpu.VMEM((heads * nblk, rows, rows), jnp.float32),
            pltpu.VMEM((rows, width), jnp.bfloat16),
            pltpu.SemaphoreType.DMA((nblk + 2,)),
        ],
        cost_estimate=pl.CostEstimate(
            flops=flops,
            transcendentals=heads * rows * rows * nblk,
            bytes_accessed=sum(b.size * 2 for b in blocks) + q.size * 2 + w_out.size * 2 + rows * out_width * 2,
        ),
    )(q, w_out, *blocks)


def layer_norm(activations, norm_gain):
    activations = activations.astype(jnp.float32)
    row_mean = jnp.mean(activations, axis=-1, keepdims=True)
    centered = activations - row_mean
    variance = jnp.mean(centered * centered, axis=-1, keepdims=True)
    return centered * lax.rsqrt(variance + EPS) * norm_gain


def body(
    tokens,
    first_gain,
    w_query,
    w_key,
    w_value,
    w_out,
    segment_ids,
    keep_mask,
    merge_gain,
    w_merge,
    merge_index,
    destination,
):
    row_count = tokens.shape[0]
    local_width = w_query.shape[1]
    heads_here = local_width // HD
    tp_size = lax.axis_size("tp")
    seq_size = lax.axis_size("seq")
    position = lax.axis_index("tp")
    seq_index = lax.axis_index("seq")

    gathered = lax.all_gather(tokens, "tp", axis=1, tiled=True)

    normed = layer_norm(gathered, first_gain).astype(jnp.bfloat16)
    queries = jnp.dot(normed, w_query, preferred_element_type=jnp.float32).astype(jnp.bfloat16)
    key_rows = jnp.dot(normed, w_key, preferred_element_type=jnp.float32).astype(jnp.bfloat16)
    value_rows = jnp.dot(normed, w_value, preferred_element_type=jnp.float32).astype(jnp.bfloat16)
    code_query = segment_ids + 1
    code_key = jnp.where(keep_mask > 0, code_query, 0)
    pair_width = 2 * local_width
    local_index = merge_index - seq_index * row_count
    order = local_index.T.reshape(row_count)
    code_rows = jnp.stack([code_key, code_query, order]).astype(jnp.bfloat16)
    code_block = jnp.zeros((8, pair_width), jnp.bfloat16)
    code_block = code_block.at[0:3, :row_count].set(code_rows)
    paired = jnp.concatenate([jnp.concatenate([key_rows, value_rows], axis=1), code_block], axis=0)
    pair_list = [paired]
    for offset in (1, 2, -1, -2):
        pair_list.append(from_behind(paired, "seq", offset))
    partial_sum = attention(queries, w_out, pair_list)
    chunk = row_count // tp_size
    pieces = lax.all_to_all(partial_sum, "tp", 0, 0, tiled=True)
    mixed_sum = jnp.sum(pieces.reshape(tp_size, chunk, -1).astype(jnp.float32), axis=0)
    column = lax.dynamic_slice_in_dim(local_index, position, 1, 1)[:, 0]
    residual = jnp.take(gathered, column, axis=0)
    updated = residual.astype(jnp.float32) + mixed_sum
    picked = layer_norm(updated, merge_gain).astype(jnp.bfloat16)
    partial_proj = jnp.dot(picked, w_merge, preferred_element_type=jnp.float32)
    partial_proj = partial_proj.astype(jnp.bfloat16)
    width = partial_proj.shape[1] // tp_size
    proj_pieces = lax.all_to_all(partial_proj, "tp", 1, 0, tiled=True)
    projected = jnp.sum(proj_pieces.reshape(tp_size, chunk, width).astype(jnp.float32), axis=0)
    projected = projected.astype(jnp.bfloat16)
    slot_count = projected.shape[0]

    owner = destination // slot_count
    slot = destination - owner * slot_count
    lane = jnp.arange(slot_count)
    same_owner = owner[:, None] == owner[None, :]
    earlier = lane[None, :] < lane[:, None]
    rank = jnp.sum(jnp.where(same_owner & earlier, 1, 0), axis=1)
    send_pos = owner * CAP + rank
    target = jnp.arange(seq_size * CAP)
    send_hot = (send_pos[None, :] == target[:, None]).astype(jnp.bfloat16)
    send_rows = jnp.dot(send_hot, projected, preferred_element_type=jnp.float32)
    send_rows = send_rows.astype(jnp.bfloat16).reshape(seq_size, CAP * width)
    slot_code = (slot + 1).astype(jnp.float32)
    send_slot = jnp.dot(send_hot.astype(jnp.float32), slot_code, precision=lax.Precision.HIGHEST)
    strip = 16
    slot_strip = jnp.zeros((seq_size, strip), jnp.bfloat16)
    slot_strip = slot_strip.at[:, :CAP].set(send_slot.reshape(seq_size, CAP).astype(jnp.bfloat16))
    send_buf = jnp.concatenate([send_rows, slot_strip], axis=1)
    recv = lax.all_to_all(send_buf, "seq", 0, 0, tiled=True)
    recv_rows = recv[:, :CAP * width].reshape(seq_size * CAP, width)
    recv_slot = recv[:, CAP * width:CAP * width + CAP].reshape(seq_size * CAP).astype(jnp.int32) - 1
    recv_hot = (recv_slot[None, :] == lane[:, None]).astype(jnp.bfloat16)
    delivered = jnp.dot(recv_hot, recv_rows, preferred_element_type=jnp.float32)
    return delivered.astype(jnp.bfloat16)


def solution(mesh):
    return jax.shard_map(
        body,
        mesh=mesh,
        in_specs=(
            P("seq", "tp"),
            P(),
            P(None, "tp"),
            P(None, "tp"),
            P(None, "tp"),
            P("tp", None),
            P("seq"),
            P("seq"),
            P(),
            P("tp", None),
            P("seq", None),
            P("seq"),
        ),
        out_specs=P("seq", "tp"),
        check_vma=False,
    )
```

```python
import functools

import jax
import jax.numpy as jnp
from jax import lax
from jax.experimental import pallas as pl
from jax.experimental.pallas import tpu as pltpu
from jax.sharding import PartitionSpec as P

HD = 80
CAP = 2


EPS = 1e-06


def from_behind(shard, axis, by):
    length = lax.axis_size(axis)
    pairs = [(i, i + by) for i in range(length) if 0 <= i + by < length]
    return lax.ppermute(shard, axis, pairs)


def attn_kernel(heads, rows, q_hbm, w_hbm, b0, b1, b2, b3, b4, out_ref,
                q_ref, w_ref, blk_ref, score_ref, att_ref, sems):
    sources = (b0, b1, b2, b3, b4)
    nblk = len(sources)
    scale = HD ** (-0.5)
    width = heads * HD
    copies = [pltpu.make_async_copy(sources[0], blk_ref.at[0], sems.at[0]),
              pltpu.make_async_copy(q_hbm, q_ref, sems.at[nblk])]
    copies += [pltpu.make_async_copy(sources[b], blk_ref.at[b], sems.at[b]) for b in range(1, nblk)]
    copies.append(pltpu.make_async_copy(w_hbm, w_ref, sems.at[nblk + 1]))
    for c in copies:
        c.start()
    copies[0].wait()
    copies[1].wait()
    side = jnp.transpose(blk_ref[0, rows:rows + 8, 0:rows].astype(jnp.float32))
    qcode = side[:, 1:2]
    order = side[:, 2:3]
    row_id = lax.broadcasted_iota(jnp.int32, (rows, rows), 0)
    col_id = lax.broadcasted_iota(jnp.int32, (rows, rows), 1)
    diag = row_id == col_id
    row_max = [None] * heads
    for b in range(nblk):
        if b >= 1:
            copies[b + 1].wait()
        kcode = blk_ref[b, rows:rows + 1, 0:rows].astype(jnp.float32)
        mask = qcode == kcode
        if b == 0:
            mask = mask | diag
        for h in range(heads):
            q = q_ref[:, h * HD:(h + 1) * HD]
            k = blk_ref[b, 0:rows, h * HD:(h + 1) * HD]
            s = lax.dot_general(q, k, (((1,), (1,)), ((), ())), preferred_element_type=jnp.float32) * scale
            s = jnp.where(mask, s, -1e30)
            score_ref[h * nblk + b] = s
            m = s.max(axis=1, keepdims=True)
            row_max[h] = m if row_max[h] is None else jnp.maximum(row_max[h], m)
    for h in range(heads):
        exps = [jnp.exp(score_ref[h * nblk + b] - row_max[h]) for b in range(nblk)]
        total = exps[0].sum(axis=1, keepdims=True)
        for e in exps[1:]:
            total = total + e.sum(axis=1, keepdims=True)
        acc = None
        for b in range(nblk):
            w = (exps[b] / total).astype(jnp.bfloat16)
            v = blk_ref[b, 0:rows, width + h * HD:width + (h + 1) * HD]
            p = jnp.dot(w, v, preferred_element_type=jnp.float32)
            acc = p if acc is None else acc + p
        att_ref[:, h * HD:(h + 1) * HD] = acc.astype(jnp.bfloat16)
    pick = (order == col_id.astype(jnp.float32)).astype(jnp.bfloat16)
    ordered = jnp.dot(pick, att_ref[...], preferred_element_type=jnp.float32)
    copies[-1].wait()
    mixed = jnp.dot(ordered.astype(jnp.bfloat16), w_ref[...], preferred_element_type=jnp.float32)
    out_ref[...] = mixed.astype(out_ref.dtype)


def attention(q, w_out, blocks):
    rows, width = q.shape
    heads = width // HD
    out_width = w_out.shape[1]
    nblk = len(blocks)
    anywhere = pl.BlockSpec(memory_space=pl.ANY)
    flops = 2 * 2 * heads * rows * rows * nblk * HD
    flops += 2 * rows * rows * width + 2 * rows * width * out_width
    return pl.pallas_call(
        functools.partial(attn_kernel, heads, rows),
        out_shape=jax.ShapeDtypeStruct((rows, out_width), jnp.bfloat16),
        in_specs=[anywhere] * (2 + nblk),
        out_specs=pl.BlockSpec(memory_space=pltpu.VMEM),
        scratch_shapes=[
            pltpu.VMEM(q.shape, jnp.bfloat16),
            pltpu.VMEM(w_out.shape, jnp.bfloat16),
            pltpu.VMEM((nblk,) + blocks[0].shape, jnp.bfloat16),
            pltpu.VMEM((heads * nblk, rows, rows), jnp.float32),
            pltpu.VMEM((rows, width), jnp.bfloat16),
            pltpu.SemaphoreType.DMA((nblk + 2,)),
        ],
        cost_estimate=pl.CostEstimate(
            flops=flops,
            transcendentals=heads * rows * rows * nblk,
            bytes_accessed=sum(b.size * 2 for b in blocks) + q.size * 2 + w_out.size * 2 + rows * out_width * 2,
        ),
    )(q, w_out, *blocks)


def layer_norm(activations, norm_gain):
    activations = activations.astype(jnp.float32)
    row_mean = jnp.mean(activations, axis=-1, keepdims=True)
    centered = activations - row_mean
    variance = jnp.mean(centered * centered, axis=-1, keepdims=True)
    return centered * lax.rsqrt(variance + EPS) * norm_gain


def body(
    tokens,
    first_gain,
    w_query,
    w_key,
    w_value,
    w_out,
    segment_ids,
    keep_mask,
    merge_gain,
    w_merge,
    merge_index,
    destination,
):
    row_count = tokens.shape[0]
    local_width = w_query.shape[1]
    heads_here = local_width // HD
    tp_size = lax.axis_size("tp")
    seq_size = lax.axis_size("seq")
    position = lax.axis_index("tp")
    seq_index = lax.axis_index("seq")

    gathered = lax.all_gather(tokens, "tp", axis=1, tiled=True)

    normed = layer_norm(gathered, first_gain).astype(jnp.bfloat16)
    queries = jnp.dot(normed, w_query, preferred_element_type=jnp.float32).astype(jnp.bfloat16)
    key_rows = jnp.dot(normed, w_key, preferred_element_type=jnp.float32).astype(jnp.bfloat16)
    value_rows = jnp.dot(normed, w_value, preferred_element_type=jnp.float32).astype(jnp.bfloat16)
    code_query = segment_ids + 1
    code_key = jnp.where(keep_mask > 0, code_query, 0)
    pair_width = 2 * local_width
    local_index = merge_index - seq_index * row_count
    order = local_index.T.reshape(row_count)
    code_rows = jnp.stack([code_key, code_query, order]).astype(jnp.bfloat16)
    code_block = jnp.zeros((8, pair_width), jnp.bfloat16)
    code_block = code_block.at[0:3, :row_count].set(code_rows)
    paired = jnp.concatenate([jnp.concatenate([key_rows, value_rows], axis=1), code_block], axis=0)
    pair_list = [paired]
    for offset in (1, -1, 2, -2):
        pair_list.append(from_behind(paired, "seq", offset))
    partial_sum = attention(queries, w_out, pair_list)
    chunk = row_count // tp_size
    pieces = lax.all_to_all(partial_sum, "tp", 0, 0, tiled=True)
    mixed_sum = jnp.sum(pieces.reshape(tp_size, chunk, -1).astype(jnp.float32), axis=0)
    column = lax.dynamic_slice_in_dim(local_index, position, 1, 1)[:, 0]
    residual = jnp.take(gathered, column, axis=0)
    updated = residual.astype(jnp.float32) + mixed_sum
    picked = layer_norm(updated, merge_gain).astype(jnp.bfloat16)
    partial_proj = jnp.dot(picked, w_merge, preferred_element_type=jnp.float32)
    partial_proj = partial_proj.astype(jnp.bfloat16)
    width = partial_proj.shape[1] // tp_size
    proj_pieces = lax.all_to_all(partial_proj, "tp", 1, 0, tiled=True)
    projected = jnp.sum(proj_pieces.reshape(tp_size, chunk, width).astype(jnp.float32), axis=0)
    projected = projected.astype(jnp.bfloat16)
    slot_count = projected.shape[0]

    owner = destination // slot_count
    slot = destination - owner * slot_count
    lane = jnp.arange(slot_count)
    same_owner = owner[:, None] == owner[None, :]
    earlier = lane[None, :] < lane[:, None]
    rank = jnp.sum(jnp.where(same_owner & earlier, 1, 0), axis=1)
    send_pos = owner * CAP + rank
    target = jnp.arange(seq_size * CAP)
    send_hot = (send_pos[None, :] == target[:, None]).astype(jnp.bfloat16)
    send_rows = jnp.dot(send_hot, projected, preferred_element_type=jnp.float32)
    send_rows = send_rows.astype(jnp.bfloat16).reshape(seq_size, CAP, width)
    slot_code = (slot + 1).astype(jnp.float32)
    send_slot = jnp.dot(send_hot.astype(jnp.float32), slot_code, precision=lax.Precision.HIGHEST)
    slot_row = jnp.zeros((seq_size, 1, width), jnp.bfloat16)
    slot_row = slot_row.at[:, 0, :CAP].set(send_slot.reshape(seq_size, CAP).astype(jnp.bfloat16))
    send_buf = jnp.concatenate([send_rows, slot_row], axis=1).reshape(seq_size * (CAP + 1), width)
    recv = lax.all_to_all(send_buf, "seq", 0, 0, tiled=True).reshape(seq_size, CAP + 1, width)
    recv_rows = recv[:, :CAP, :].reshape(seq_size * CAP, width)
    recv_slot = recv[:, CAP, :CAP].reshape(seq_size * CAP).astype(jnp.int32) - 1
    recv_hot = (recv_slot[None, :] == lane[:, None]).astype(jnp.bfloat16)
    delivered = jnp.dot(recv_hot, recv_rows, preferred_element_type=jnp.float32)
    return delivered.astype(jnp.bfloat16)


def solution(mesh):
    return jax.shard_map(
        body,
        mesh=mesh,
        in_specs=(
            P("seq", "tp"),
            P(),
            P(None, "tp"),
            P(None, "tp"),
            P(None, "tp"),
            P("tp", None),
            P("seq"),
            P("seq"),
            P(),
            P("tp", None),
            P("seq", None),
            P("seq"),
        ),
        out_specs=P("seq", "tp"),
        check_vma=False,
    )
```
